512 devices in a mesh: gx: 8 (over y), gy: 16 (over z_hi, x, core), gz: 4 (over z_lo).
Axes of the slice: x: 4, y: 8, z: 8 (z_hi: 2, z_lo: 4; z = z_hi * 4 + z_lo), core: 2. Of those that a mesh axis runs over, the one named last changes fastest.
Arguments:
- features: bfloat16 [8, 64, 128, 256], P('gx', 'gy', 'gz'), may hold values from -6 to 6
- neighbour_code: int32 [8, 64, 128, 64], P('gx', 'gy', 'gz'), may hold values from 0 to 107, as said below
- distance: float32 [8, 64, 128, 64], P('gx', 'gy', 'gz'), may hold values from 0.8 to 4.8
- w_message: bfloat16 [2, 2048, 256], replicated, may hold values from -0.125 to 0.125
- w_update: bfloat16 [2, 256, 256], replicated, may hold values from -0.375 to 0.375
- norm_gain: float32 [2, 256], replicated, may hold values from 0.1 to 1.9
- w_env: bfloat16 [256, 128], replicated, may hold values from -0.375 to 0.375
- w_out: bfloat16 [3, 256], replicated, may hold values from -0.375 to 0.375
- w_first: bfloat16 [128, 128, 1024], P(('gx', 'gy')), may hold values from -0.5 to 0.5
- w_head: bfloat16 [128, 3, 1024], P(('gx', 'gy')), may hold values from -0.75 to 0.75
- flag_ids: int32 [8, 16, 4, 32], P('gx', 'gy', 'gz'), may hold values from 0 to 127, as said below
- flag_owner: int32 [8, 16, 4, 32, 1], P('gx', 'gy', 'gz'), may hold values from 0 to 127; in each aligned block of 32 rows (0 to 31, 32 to 63, ..., all dimensions but the last counted through in order) at most 2 rows name the same one
- flag_count: int32 [8, 16, 4], P('gx', 'gy', 'gz'), may hold values from 24 to 32, as said below
Outputs:
- forces: float32 [3, 8, 64, 128], P(None, 'gx', 'gy', 'gz')
The draws below stay inside these ranges and needn't reach their ends.
Inputs may be any that keep to these rules, and one draw needn't show every extreme that they name: `neighbour_code`: an atom's 64 codes are distinct and never name the atom itself (code 13 * 4 + its position along the thickness mod 4). `flag_ids`: the 32 indices of one device are distinct. `flag_owner`: of the 32 rows of one device, live or not, at most 2 name the same specialist, and some device has 2 rows naming one. Rows 0 to flag_count - 1 of a device are live; some device has all 32 live.
All inputs are finite; a program needn't handle non-finite values.
Results may differ from the reference program's by a relative error of at most 0.0085.
Values may be sent and summed in bfloat16 or wider, within the bound.
No kernel may reach another device: no remote copies, remote signals or barrier semaphores. Data moves between devices by JAX's collectives and lax.ppermute only.
A program may use at most 64 MiB of HBM per device.

```python
import math
import jax
import jax.numpy as jnp
import numpy as np
from jax import lax

CX = 1
CY = 4
CZ = 8
M = 4
K = 64
F = 256
NRB = 8
L = 2
E = 128
HF = 1024
FLAG_DEV = 32
NOWN = 128
CAP = 2
NX = 8
NY = 64
ZM = 128
ATOMS_DEV = 128
N_GX = 8
N_GY = 16
N_GZ = 4


def draw_neighbour_code(key, part):
    candidates = 27 * M
    scores = jax.random.randint(key, (NX, NY, ZM, candidates), 0, 1 << 20) * candidates + jnp.arange(candidates, dtype=jnp.int32)
    self_code = 13 * M + jnp.arange(ZM, dtype=jnp.int32) % M
    scores = jnp.where(jnp.arange(candidates, dtype=jnp.int32)[None, None, None, :] == self_code[None, None, :, None], -1, scores)
    return lax.top_k(scores, K)[1].astype(jnp.int32)


def draw_flag_ids(key, part):
    device_keys = jax.random.split(key, N_GX * N_GY * N_GZ)
    chosen = jax.vmap(lambda single: jax.random.permutation(single, ATOMS_DEV)[:FLAG_DEV])(device_keys)
    return chosen.reshape(N_GX, N_GY, N_GZ, FLAG_DEV).astype(jnp.int32)


def draw_flag_count(key, part):
    counts = jax.random.randint(key, (N_GX, N_GY, N_GZ), 3 * FLAG_DEV // 4, FLAG_DEV + 1)
    return jnp.where(counts == jnp.max(counts), FLAG_DEV, counts).astype(jnp.int32)


def block_levels(own_key, extent, pieces, least, top_value):
    def one(dim, blocks):
        heights = jax.random.uniform(jax.random.fold_in(jax.random.fold_in(own_key, 6), dim), (blocks,), jnp.float32, least / len(pieces), top_value / len(pieces))
        return jnp.repeat(jnp.exp(heights), extent[dim] // blocks).reshape((-1,) + (1,) * (len(extent) - dim - 1))

    level = one(*pieces[0])
    for cut in pieces[1:]:
        level = level * one(*cut)
    return level


def shared_out(own_key, own, number, rows, number_of, top, limit, skew):
    ranking = jax.random.permutation(own_key, number_of)
    heavy_load, usual = load_shares(number_of, rows * top, limit, skew, True), load_shares(number_of, rows * top, limit, skew, False)
    places = jnp.arange(number_of)

    def named(tallies, offset_by):
        used = int((tallies > 0).sum())
        fixed = max(1, used // 4)
        shifted = fixed + (places - fixed + offset_by * (used - fixed)) % max(1, number_of - fixed)
        return jnp.zeros((number_of,), jnp.int32).at[ranking[jnp.where(places < fixed, places, shifted)]].set(jnp.asarray(tallies, jnp.int32))

    tallies = jnp.where(number % 4 == 0, named(heavy_load, number // 4), named(usual, number - number // 4 - 1))
    mixed = jax.random.permutation(jax.random.fold_in(own, 3), number_of)
    donor, sink = mixed[0:number_of // 2 * 2:2], mixed[1:number_of // 2 * 2:2]
    slack = jnp.minimum(tallies[donor] - 1, limit - tallies[sink]) // 2
    slack = jnp.where((donor == ranking[0]) | (sink == ranking[0]) | (tallies[sink] == 0), 0, jnp.maximum(slack, 0))
    shifted = jax.random.randint(jax.random.fold_in(own, 4), (number_of // 2,), 0, 1 << 20) % (slack + 1)
    tallies = tallies.at[donor].add(-shifted).at[sink].add(shifted)
    items = jnp.searchsorted(jnp.cumsum(tallies), jnp.arange(rows * top), side="right").astype(jnp.int32)
    listing = items.reshape(top, rows).T
    listing = listing[jax.random.permutation(jax.random.fold_in(own, 1), rows)]
    offset_by = jax.random.randint(jax.random.fold_in(own, 2), (rows, 1), 0, top)
    return jnp.take_along_axis(listing, (jnp.arange(top)[None, :] + offset_by) % top, axis=1)


def load_shares(count, total, most, skew, full):
    loads = [(1 << 20) // math.isqrt(rank ** skew) + 1 for rank in range(1, count + 1)]
    largest = most if full else min(most, max(-(-total // count), total * loads[0] // sum(loads)))
    least = 1 if total - largest >= count - 1 else 0
    given, rest = [largest] + [least] * (count - 1), total - largest - least * (count - 1)
    while rest > 0:
        free = [i for i in range(1, count) if given[i] < largest] or [i for i in range(1, count) if given[i] < most]
        whole, left = sum([loads[i] for i in free]), rest
        for i in free:
            more = min(most - given[i], max(1, left * loads[i] // whole), rest)
            given[i] = given[i] + more
            rest = rest - more
    return np.array(given)


def scatter_about(rng, extent, width, reach, shards=(), held_as=jnp.bfloat16):
    array = width * jax.random.normal(rng, extent, jnp.float32)
    if shards:
        array = array * block_levels(rng, extent, shards, -0.22, 0.18)
    return jnp.clip(array, -reach, reach).astype(held_as)


def setup_inputs(seed: int = 0) -> dict:
    keys = jax.random.split(jax.random.key(seed), 14)
    features = scatter_about(keys[0], (NX, NY, ZM, F), 1.0, 6.0, ((0, 8), (1, 16), (2, 4)))
    neighbour_code = draw_neighbour_code(jax.random.fold_in(keys[13], 71), 0)
    distance = jnp.clip(0.8 + 4 * jax.random.uniform(keys[2], (NX, NY, ZM, K), jnp.float32) ** block_levels(keys[2], (NX, NY, ZM, K), ((0, 8), (1, 16), (2, 4)), -0.2, 0.2), 0.8, 4.8)
    w_message = scatter_about(keys[3], (L, NRB * F, F), (NRB * F) ** -0.5, 0.125)
    w_update = scatter_about(keys[4], (L, F, F), F ** -0.5, 0.375)
    norm_gain = jnp.clip(1.0 + 0.18 * jax.random.normal(keys[5], (L, F), jnp.float32), 0.1, 1.9)
    w_env = scatter_about(keys[6], (F, E), F ** -0.5, 0.375)
    w_out = scatter_about(keys[7], (3, F), F ** -0.5, 0.375)
    w_first = scatter_about(keys[8], (NOWN, E, HF), E ** -0.5, 0.5, ((0, 128),))
    w_head = scatter_about(keys[9], (NOWN, 3, HF), 0.125, 0.75, ((0, 128),))
    flag_ids = draw_flag_ids(jax.random.fold_in(keys[13], 71), 0)
    flag_owner_keys = jax.random.split(jax.random.fold_in(keys[11], 1), N_GX * N_GY * N_GZ * FLAG_DEV // FLAG_DEV)
    flag_owner_turns = jax.random.permutation(jax.random.fold_in(keys[11], 3), N_GX * N_GY * N_GZ * FLAG_DEV // FLAG_DEV)
    flag_owner = jax.vmap(lambda own, number: shared_out(jax.random.fold_in(keys[11], 2), own, number, FLAG_DEV, NOWN, 1, CAP, 2))(flag_owner_keys, flag_owner_turns).reshape((N_GX, N_GY, N_GZ, FLAG_DEV, 1))
    flag_count = draw_flag_count(jax.random.fold_in(keys[13], 71), 0)
    return dict(features=features, neighbour_code=neighbour_code, distance=distance, w_message=w_message, w_update=w_update, norm_gain=norm_gain, w_env=w_env, w_out=w_out, w_first=w_first, w_head=w_head, flag_ids=flag_ids, flag_owner=flag_owner, flag_count=flag_count)


CUTOFF_RADIUS = 5.0
WIDTH_GAMMA = 2.0

def radial(distance):
    cutoff = 0.5 * (jnp.cos(jnp.pi * distance / CUTOFF_RADIUS) + 1.0)
    centres = 0.8 + jnp.arange(NRB).astype(distance.dtype) * (4.0 / (NRB - 1))
    radial_basis = jnp.exp(-WIDTH_GAMMA * (distance[..., None] - centres) ** 2) * cutoff[..., None]
    return (radial_basis.astype(jnp.bfloat16), cutoff)

def neighbour_rows(codes, coord_x, coord_y, coord_z, span_y, span_z):
    offset = codes // M
    within = codes % M
    step_x = offset // 9 - 1
    step_y = offset // 3 % 3 - 1
    step_z = offset % 3 - 1
    return ((coord_x + 1 + step_x) * span_y + (coord_y + 1 + step_y)) * span_z + (coord_z // M + 1 + step_z) * M + within

def update(state, summed, w_message, w_update, gain):
    message = jnp.dot(summed, w_message, preferred_element_type=jnp.float32)
    active = jax.nn.silu(message).astype(jnp.bfloat16)
    residual = state.astype(jnp.float32) + jnp.dot(active, w_update, preferred_element_type=jnp.float32)
    inv_rms = lax.rsqrt(lax.optimization_barrier(jnp.mean(residual * residual, axis=-1, keepdims=True)) + 1e-06)
    return (residual * inv_rms * gain).astype(jnp.bfloat16)

def pad_global(values):
    values = jnp.pad(values, ((1, 1), (1, 1), (0, 0), (0, 0)), mode='wrap')
    return jnp.pad(values, ((0, 0), (0, 0), (M, M), (0, 0)))

def cheap_layer(state, neighbour_code, radial_basis, w_message, w_update, gain):
    flat_rows = pad_global(state).reshape(-1, state.shape[-1])
    span_y = NY + 2
    span_z = ZM + 2 * M
    coord_z = jnp.arange(ZM, dtype=jnp.int32)[:, None]

    def one_line(line):
        coord_x = line // NY
        coord_y = line % NY
        row_index = neighbour_rows(neighbour_code[coord_x, coord_y], coord_x, coord_y, coord_z, span_y, span_z)
        nearby = flat_rows[row_index]
        summed = jnp.einsum('zsk,zsf->zkf', radial_basis[coord_x, coord_y].astype(jnp.float32), nearby.astype(jnp.float32))
        summed = summed.reshape(ZM, -1).astype(jnp.bfloat16)
        return update(state[coord_x, coord_y], summed, w_message, w_update, gain)
    lines = lax.map(one_line, jnp.arange(NX * NY, dtype=jnp.int32))
    return lines.reshape(state.shape)

def reference(features, neighbour_code, distance, w_message, w_update, norm_gain, w_env, w_out, w_first, w_head, flag_ids, flag_owner, flag_count):
    radial_basis, cutoff = radial(distance)
    state = features
    for layer_index in range(L):
        state = cheap_layer(state, neighbour_code, radial_basis, w_message[layer_index], w_update[layer_index], norm_gain[layer_index])
    flat_state = state.reshape(-1, F)
    projected = jnp.dot(flat_state, w_env, preferred_element_type=jnp.float32).astype(jnp.bfloat16)
    flat_proj = pad_global(projected.reshape(NX, NY, ZM, E)).reshape(-1, E)
    base_force = jnp.einsum('af,cf->ca', flat_state.astype(jnp.float32), w_out.astype(jnp.float32)).reshape(3, NX, NY, ZM)
    span_y = NY + 2
    span_z = ZM + 2 * M
    depth = CZ * M

    def one_device(device):
        index_x = device // (N_GY * N_GZ)
        index_y = device // N_GZ % N_GY
        index_z = device % N_GZ
        local_ids = flag_ids[index_x, index_y, index_z]
        owner = flag_owner[index_x, index_y, index_z, :, 0]
        count = flag_count[index_x, index_y, index_z]
        pos_x = (index_x * CX + local_ids // (CY * depth)).astype(jnp.int32)
        pos_y = (index_y * CY + local_ids // depth % CY).astype(jnp.int32)
        pos_z = (index_z * depth + local_ids % depth).astype(jnp.int32)
        codes = neighbour_code[pos_x, pos_y, pos_z]
        row_index = neighbour_rows(codes, pos_x[:, None], pos_y[:, None], pos_z[:, None], span_y, span_z)
        nearby = flat_proj[row_index]
        environ = (cutoff[pos_x, pos_y, pos_z][..., None] * nearby.astype(jnp.float32)).astype(jnp.bfloat16)
        hidden = jax.nn.silu(jnp.einsum('rse,reh->rsh', environ.astype(jnp.float32), w_first[owner].astype(jnp.float32))).astype(jnp.bfloat16)
        pooled = (lax.optimization_barrier(jnp.sum(hidden.astype(jnp.float32), axis=1)) / K).astype(jnp.bfloat16)
        force = jnp.einsum('rh,rch->rc', pooled.astype(jnp.float32), w_head[owner].astype(jnp.float32))
        alive = (jnp.arange(FLAG_DEV, dtype=jnp.int32) < count).astype(force.dtype)
        return (force * alive[:, None], pos_x, pos_y, pos_z)
    correction, pos_x, pos_y, pos_z = lax.map(one_device, jnp.arange(N_GX * N_GY * N_GZ, dtype=jnp.int32))
    correction = correction.reshape(-1, 3)
    return base_force.at[:, pos_x.reshape(-1), pos_y.reshape(-1), pos_z.reshape(-1)].add(correction.T)
```

```python
import math

import jax
import jax.numpy as jnp
from jax import lax
from jax.sharding import PartitionSpec as P

M = 4
NRB = 8
L = 2


CUTOFF_RADIUS = 5.0
WIDTH_GAMMA = 2.0


def with_halo(cells, sides, width, closed):
    for axis, dim in sides:
        count = lax.axis_size(axis)
        ends = count if closed else count - 1
        head = lax.slice_in_dim(cells, 0, width, axis=dim)
        tail = lax.slice_in_dim(cells, cells.shape[dim] - width, cells.shape[dim], axis=dim)
        cells = jnp.concatenate(
            [
                lax.ppermute(tail, axis, [(i, (i + 1) % count) for i in range(ends)]),
                cells,
                lax.ppermute(head, axis, [((i + 1) % count, i) for i in range(ends)]),
            ],
            axis=dim,
        )
    return cells


def radial(distance):
    cutoff = 0.5 * (jnp.cos(jnp.pi * distance / CUTOFF_RADIUS) + 1.0)
    centres = 0.8 + jnp.arange(NRB).astype(distance.dtype) * (4.0 / (NRB - 1))
    radial_basis = jnp.exp(-WIDTH_GAMMA * (distance[..., None] - centres) ** 2) * cutoff[..., None]
    return (radial_basis.astype(jnp.bfloat16), cutoff)


def neighbour_rows(codes, coord_x, coord_y, coord_z, span_y, span_z):
    offset = codes // M
    within = codes % M
    step_x = offset // 9 - 1
    step_y = offset // 3 % 3 - 1
    step_z = offset % 3 - 1
    return (
        ((coord_x + 1 + step_x) * span_y + (coord_y + 1 + step_y)) * span_z
        + (coord_z // M + 1 + step_z) * M
        + within
    )


def update(state, summed, w_message, w_update, gain):
    message = jnp.dot(summed, w_message, preferred_element_type=jnp.float32)
    active = jax.nn.silu(message).astype(jnp.bfloat16)
    residual = state.astype(jnp.float32) + jnp.dot(
        active, w_update, preferred_element_type=jnp.float32
    )
    inv_rms = lax.rsqrt(jnp.mean(residual * residual, axis=-1, keepdims=True) + 1e-06)
    return (residual * inv_rms * gain).astype(jnp.bfloat16)


def ghosts(values):
    deeper = with_halo(values, (("gz", 2),), M, False)
    return with_halo(deeper, (("gx", 0), ("gy", 1)), 1, True)


def candidates(padded, cells_x, cells_y, cells_z):
    feature_width = padded.shape[-1]
    pieces = []
    for step_x in range(3):
        for step_y in range(3):
            for step_z in range(3):
                piece = padded[
                    step_x : step_x + cells_x,
                    step_y : step_y + cells_y,
                    step_z * M : step_z * M + cells_z * M,
                ]
                pieces.append(piece.reshape(cells_x, cells_y, cells_z, M, feature_width))
    stacked = jnp.stack(pieces, axis=3)
    return stacked.reshape(cells_x * cells_y * cells_z, 27 * M, feature_width)


def cheap_layer(state, weights, w_message, w_update, gain):
    cells_x, cells_y, depth, feature_width = state.shape
    cells_z = depth // M
    cell_count = cells_x * cells_y * cells_z
    atom_count = cell_count * M
    nearby = candidates(ghosts(state), cells_x, cells_y, cells_z)
    summed = jnp.einsum(
        "bmkc,bcf->bmkf",
        weights.reshape(cell_count, M, NRB, 27 * M),
        nearby,
        preferred_element_type=jnp.float32,
    )
    summed = summed.reshape(atom_count, NRB * feature_width).astype(jnp.bfloat16)
    return update(
        state.reshape(atom_count, feature_width), summed, w_message, w_update, gain
    ).reshape(state.shape)


def specialist(received, w_first, w_head):
    sources, item_count = (received.shape[0], received.shape[1])
    env_total = sources * item_count
    block_size = math.gcd(env_total, 16)
    environs = received.reshape(env_total, received.shape[2], received.shape[3])
    flat_live = jnp.any(environs != 0, axis=(1, 2))

    def run_block(env_piece):
        hidden = jax.nn.silu(
            jnp.einsum("bse,eh->bsh", env_piece, w_first, preferred_element_type=jnp.float32)
        ).astype(jnp.bfloat16)
        pooled = (jnp.sum(hidden, axis=1, dtype=jnp.float32) / hidden.shape[1]).astype(jnp.bfloat16)
        return jnp.einsum("bh,ch->bc", pooled, w_head, preferred_element_type=jnp.float32)

    order = jnp.argsort(jnp.where(flat_live, 0, 1).astype(jnp.int32), stable=True)
    live_total = jnp.sum(flat_live.astype(jnp.int32))
    ordered = environs[order]
    block_count = (live_total + block_size - 1) // block_size

    def step_block(index, gathered):
        offset = index * block_size
        piece = lax.dynamic_slice_in_dim(ordered, offset, block_size, 0)
        return lax.dynamic_update_slice_in_dim(gathered, run_block(piece), offset, 0)

    sorted_results = lax.fori_loop(
        0, block_count, step_block, jnp.zeros((env_total, 3), jnp.float32)
    )
    results = jnp.zeros((env_total, 3), jnp.float32).at[order].set(sorted_results)
    results = results * flat_live[:, None].astype(jnp.float32)
    return results.reshape(sources, item_count, 3)


def per_device(
    features,
    neighbour_code,
    distance,
    w_message,
    w_update,
    norm_gain,
    w_env,
    w_out,
    w_first,
    w_head,
    flag_ids,
    flag_owner,
    flag_count,
):
    cells_x, cells_y, depth, feature_width = features.shape
    cells_z = depth // M
    atom_count = cells_x * cells_y * depth
    codes = neighbour_code.reshape(atom_count, -1)
    radial_basis, cutoff = radial(distance.reshape(atom_count, -1))
    code_range = jnp.arange(27 * M, dtype=jnp.int32)
    onehot = (codes[:, :, None] == code_range[None, None, :]).astype(jnp.bfloat16)
    weights = jnp.einsum(
        "ask,asc->akc", radial_basis, onehot, preferred_element_type=jnp.float32
    ).astype(jnp.bfloat16)
    state = features
    for layer_index in range(L):
        state = cheap_layer(
            state,
            weights,
            w_message[layer_index],
            w_update[layer_index],
            norm_gain[layer_index],
        )
    flat_state = state.reshape(atom_count, feature_width)
    projected = jnp.dot(flat_state, w_env, preferred_element_type=jnp.float32).astype(jnp.bfloat16)
    env_width = projected.shape[-1]
    proj_near = candidates(
        ghosts(projected.reshape(cells_x, cells_y, depth, env_width)), cells_x, cells_y, cells_z
    )
    base_force = jnp.einsum("af,cf->ca", flat_state, w_out, preferred_element_type=jnp.float32)
    local_ids = flag_ids.reshape(-1)
    owner = flag_owner.reshape(-1)
    flag_total = local_ids.shape[0]
    live_rows = jnp.arange(flag_total, dtype=jnp.int32) < flag_count.reshape(())
    picked = jnp.einsum(
        "rsc,rce->rse",
        onehot[local_ids],
        proj_near[local_ids // M],
        preferred_element_type=jnp.float32,
    )
    environ = (cutoff[local_ids][..., None] * picked).astype(jnp.bfloat16)
    slots = environ.shape[1]
    owner_total = lax.axis_size("gx") * lax.axis_size("gy")
    capacity = max(2, 2 * flag_total // owner_total)
    same = (owner[:, None] == jnp.arange(owner_total, dtype=jnp.int32)[None, :]).astype(jnp.int32)
    before = jnp.cumsum(same, axis=0) - same
    slot_index = jnp.sum(before * same, axis=1)
    target = jnp.where(live_rows, owner * capacity + slot_index, owner_total * capacity)
    placing = (
        jnp.arange(owner_total * capacity, dtype=jnp.int32)[:, None] == target[None, :]
    ).astype(jnp.bfloat16)
    outgoing = jnp.dot(
        placing, environ.reshape(flag_total, slots * env_width), preferred_element_type=jnp.float32
    ).astype(jnp.bfloat16)
    local_first = w_first[0]
    local_head = w_head[0]
    results = specialist(
        lax.all_to_all(
            outgoing.reshape(owner_total, capacity, slots, env_width),
            ("gx", "gy"),
            split_axis=0,
            concat_axis=0,
            tiled=True,
        ),
        local_first,
        local_head,
    )
    returned = lax.all_to_all(results, ("gx", "gy"), split_axis=0, concat_axis=0, tiled=True)
    returned = returned.reshape(owner_total * capacity, 3)
    correction = returned[jnp.minimum(target, owner_total * capacity - 1)] * live_rows[
        :, None
    ].astype(jnp.float32)
    forces = base_force.at[:, local_ids].add(correction.T)
    return forces.reshape(3, cells_x, cells_y, depth)


def solution(mesh):
    placed = (
        P("gx", "gy", "gz", None),
        P("gx", "gy", "gz", None),
        P("gx", "gy", "gz", None),
        P(),
        P(),
        P(),
        P(),
        P(),
        P(("gx", "gy"), None, None),
        P(("gx", "gy"), None, None),
        P("gx", "gy", "gz", None),
        P("gx", "gy", "gz", None, None),
        P("gx", "gy", "gz"),
    )
    return jax.shard_map(
        per_device, mesh=mesh, in_specs=placed, out_specs=P(None, "gx", "gy", "gz"), check_vma=False
    )
```

```python
import math

import jax
import jax.numpy as jnp
from jax import lax
from jax.sharding import PartitionSpec as P
from jax.experimental import pallas as pl

M = 4
NRB = 8
L = 2


CUTOFF_RADIUS = 5.0
WIDTH_GAMMA = 2.0


def with_halo(cells, sides, width, closed):
    for axis, dim in sides:
        count = lax.axis_size(axis)
        ends = count if closed else count - 1
        head = lax.slice_in_dim(cells, 0, width, axis=dim)
        tail = lax.slice_in_dim(cells, cells.shape[dim] - width, cells.shape[dim], axis=dim)
        cells = jnp.concatenate(
            [
                lax.ppermute(tail, axis, [(i, (i + 1) % count) for i in range(ends)]),
                cells,
                lax.ppermute(head, axis, [((i + 1) % count, i) for i in range(ends)]),
            ],
            axis=dim,
        )
    return cells


def radial(distance):
    cutoff = 0.5 * (jnp.cos(jnp.pi * distance / CUTOFF_RADIUS) + 1.0)
    centres = 0.8 + jnp.arange(NRB).astype(distance.dtype) * (4.0 / (NRB - 1))
    radial_basis = jnp.exp(-WIDTH_GAMMA * (distance[..., None] - centres) ** 2) * cutoff[..., None]
    return (radial_basis.astype(jnp.bfloat16), cutoff)


def neighbour_rows(codes, coord_x, coord_y, coord_z, span_y, span_z):
    offset = codes // M
    within = codes % M
    step_x = offset // 9 - 1
    step_y = offset // 3 % 3 - 1
    step_z = offset % 3 - 1
    return (
        ((coord_x + 1 + step_x) * span_y + (coord_y + 1 + step_y)) * span_z
        + (coord_z // M + 1 + step_z) * M
        + within
    )


def update(state, summed, w_message, w_update, gain):
    message = jnp.dot(summed, w_message, preferred_element_type=jnp.float32)
    active = jax.nn.silu(message).astype(jnp.bfloat16)
    residual = state.astype(jnp.float32) + jnp.dot(
        active, w_update, preferred_element_type=jnp.float32
    )
    inv_rms = lax.rsqrt(jnp.mean(residual * residual, axis=-1, keepdims=True) + 1e-06)
    return (residual * inv_rms * gain).astype(jnp.bfloat16)


def ghosts(values):
    deeper = with_halo(values, (("gz", 2),), M, False)
    return with_halo(deeper, (("gx", 0), ("gy", 1)), 1, True)


def candidates(padded, cells_x, cells_y, cells_z):
    feature_width = padded.shape[-1]
    pieces = []
    for step_x in range(3):
        for step_y in range(3):
            for step_z in range(3):
                piece = padded[
                    step_x : step_x + cells_x,
                    step_y : step_y + cells_y,
                    step_z * M : step_z * M + cells_z * M,
                ]
                pieces.append(piece.reshape(cells_x, cells_y, cells_z, M, feature_width))
    stacked = jnp.stack(pieces, axis=3)
    return stacked.reshape(cells_x * cells_y * cells_z, 27 * M, feature_width)


def cheap_layer(state, weights, w_message, w_update, gain):
    cells_x, cells_y, depth, feature_width = state.shape
    cells_z = depth // M
    cell_count = cells_x * cells_y * cells_z
    atom_count = cell_count * M
    nearby = candidates(ghosts(state), cells_x, cells_y, cells_z)
    summed = jnp.einsum(
        "bmkc,bcf->bmkf",
        weights.reshape(cell_count, M, NRB, 27 * M),
        nearby,
        preferred_element_type=jnp.float32,
    )
    summed = summed.reshape(atom_count, NRB * feature_width).astype(jnp.bfloat16)
    return update(
        state.reshape(atom_count, feature_width), summed, w_message, w_update, gain
    ).reshape(state.shape)


def specialist_kernel(env_ref, first_ref, head_ref, out_ref):
    piece = 8
    slots = env_ref.shape[0] // out_ref.shape[0]
    span = piece * slots
    column = lax.broadcasted_iota(jnp.int32, (piece, span), 1)
    row = lax.broadcasted_iota(jnp.int32, (piece, span), 0)
    pool = ((column >= row * slots) & (column < (row + 1) * slots)).astype(jnp.bfloat16)

    def body(index, carry):
        begin = pl.multiple_of(index * span, span)
        message = jnp.dot(
            env_ref[pl.ds(begin, span), :], first_ref[...], preferred_element_type=jnp.float32
        )
        hidden = (message * (0.5 * jnp.tanh(0.5 * message) + 0.5)).astype(jnp.bfloat16)
        pooled = jnp.dot(pool, hidden, preferred_element_type=jnp.float32)
        pooled = (pooled * (1.0 / slots)).astype(jnp.bfloat16)
        out_ref[pl.ds(pl.multiple_of(index * piece, piece), piece), :] = jnp.dot(
            pooled, head_ref[...], preferred_element_type=jnp.float32
        )
        return carry

    lax.fori_loop(0, out_ref.shape[0] // piece, body, 0)


def specialist(received, w_first, w_head):
    sources, item_count, slots, env_width = received.shape
    env_total = sources * item_count
    hidden_width = w_first.shape[-1]
    block = math.gcd(env_total, 32)
    head = jnp.zeros((hidden_width, 128), jnp.bfloat16).at[:, : w_head.shape[0]].set(w_head.T)
    results = pl.pallas_call(
        specialist_kernel,
        grid=(env_total // block,),
        in_specs=[
            pl.BlockSpec((block * slots, env_width), lambda i: (i, 0)),
            pl.BlockSpec((env_width, hidden_width), lambda i: (0, 0)),
            pl.BlockSpec((hidden_width, 128), lambda i: (0, 0)),
        ],
        out_specs=pl.BlockSpec((block, 128), lambda i: (i, 0)),
        out_shape=jax.ShapeDtypeStruct((env_total, 128), jnp.float32),
    )(received.reshape(env_total * slots, env_width), w_first, head)
    return results[:, : w_head.shape[0]].reshape(sources, item_count, w_head.shape[0])


def per_device(
    features,
    neighbour_code,
    distance,
    w_message,
    w_update,
    norm_gain,
    w_env,
    w_out,
    w_first,
    w_head,
    flag_ids,
    flag_owner,
    flag_count,
):
    cells_x, cells_y, depth, feature_width = features.shape
    cells_z = depth // M
    atom_count = cells_x * cells_y * depth
    codes = neighbour_code.reshape(atom_count, -1)
    radial_basis, cutoff = radial(distance.reshape(atom_count, -1))
    code_range = jnp.arange(27 * M, dtype=jnp.int32)
    onehot = (codes[:, :, None] == code_range[None, None, :]).astype(jnp.bfloat16)
    weights = jnp.einsum(
        "ask,asc->akc", radial_basis, onehot, preferred_element_type=jnp.float32
    ).astype(jnp.bfloat16)
    state = features
    for layer_index in range(L):
        state = cheap_layer(
            state,
            weights,
            w_message[layer_index],
            w_update[layer_index],
            norm_gain[layer_index],
        )
    flat_state = state.reshape(atom_count, feature_width)
    projected = jnp.dot(flat_state, w_env, preferred_element_type=jnp.float32).astype(jnp.bfloat16)
    env_width = projected.shape[-1]
    proj_near = candidates(
        ghosts(projected.reshape(cells_x, cells_y, depth, env_width)), cells_x, cells_y, cells_z
    )
    base_force = jnp.einsum("af,cf->ca", flat_state, w_out, preferred_element_type=jnp.float32)
    local_ids = flag_ids.reshape(-1)
    owner = flag_owner.reshape(-1)
    flag_total = local_ids.shape[0]
    live_rows = jnp.arange(flag_total, dtype=jnp.int32) < flag_count.reshape(())
    picked = jnp.einsum(
        "rsc,rce->rse",
        onehot[local_ids],
        proj_near[local_ids // M],
        preferred_element_type=jnp.float32,
    )
    environ = (cutoff[local_ids][..., None] * picked).astype(jnp.bfloat16)
    slots = environ.shape[1]
    owner_total = lax.axis_size("gx") * lax.axis_size("gy")
    capacity = max(2, 2 * flag_total // owner_total)
    same = (owner[:, None] == jnp.arange(owner_total, dtype=jnp.int32)[None, :]).astype(jnp.int32)
    before = jnp.cumsum(same, axis=0) - same
    slot_index = jnp.sum(before * same, axis=1)
    target = jnp.where(live_rows, owner * capacity + slot_index, owner_total * capacity)
    placing = (
        jnp.arange(owner_total * capacity, dtype=jnp.int32)[:, None] == target[None, :]
    ).astype(jnp.bfloat16)
    outgoing = jnp.dot(
        placing, environ.reshape(flag_total, slots * env_width), preferred_element_type=jnp.float32
    ).astype(jnp.bfloat16)
    local_first = w_first[0]
    local_head = w_head[0]
    results = specialist(
        lax.all_to_all(
            outgoing.reshape(owner_total, capacity, slots, env_width),
            ("gx", "gy"),
            split_axis=0,
            concat_axis=0,
            tiled=True,
        ),
        local_first,
        local_head,
    )
    returned = lax.all_to_all(results, ("gx", "gy"), split_axis=0, concat_axis=0, tiled=True)
    returned = returned.reshape(owner_total * capacity, 3)
    correction = returned[jnp.minimum(target, owner_total * capacity - 1)] * live_rows[
        :, None
    ].astype(jnp.float32)
    forces = base_force.at[:, local_ids].add(correction.T)
    return forces.reshape(3, cells_x, cells_y, depth)


def solution(mesh):
    placed = (
        P("gx", "gy", "gz", None),
        P("gx", "gy", "gz", None),
        P("gx", "gy", "gz", None),
        P(),
        P(),
        P(),
        P(),
        P(),
        P(("gx", "gy"), None, None),
        P(("gx", "gy"), None, None),
        P("gx", "gy", "gz", None),
        P("gx", "gy", "gz", None, None),
        P("gx", "gy", "gz"),
    )
    return jax.shard_map(
        per_device, mesh=mesh, in_specs=placed, out_specs=P(None, "gx", "gy", "gz"), check_vma=False
    )
```

```python
import math

import jax
import jax.numpy as jnp
from jax import lax
from jax.sharding import PartitionSpec as P
from jax.experimental import pallas as pl


M = 4
NRB = 8
L = 2


CUTOFF_RADIUS = 5.0
WIDTH_GAMMA = 2.0


def with_halo(cells, sides, width, closed):
    for axis, dim in sides:
        count = lax.axis_size(axis)
        ends = count if closed else count - 1
        head = lax.slice_in_dim(cells, 0, width, axis=dim)
        tail = lax.slice_in_dim(cells, cells.shape[dim] - width, cells.shape[dim], axis=dim)
        cells = jnp.concatenate(
            [
                lax.ppermute(tail, axis, [(i, (i + 1) % count) for i in range(ends)]),
                cells,
                lax.ppermute(head, axis, [((i + 1) % count, i) for i in range(ends)]),
            ],
            axis=dim,
        )
    return cells


def radial(distance):
    cutoff = 0.5 * (jnp.cos(jnp.pi * distance / CUTOFF_RADIUS) + 1.0)
    centres = 0.8 + jnp.arange(NRB).astype(distance.dtype) * (4.0 / (NRB - 1))
    radial_basis = jnp.exp(-WIDTH_GAMMA * (distance[..., None] - centres) ** 2) * cutoff[..., None]
    return (radial_basis.astype(jnp.bfloat16), cutoff)


def neighbour_rows(codes, coord_x, coord_y, coord_z, span_y, span_z):
    offset = codes // M
    within = codes % M
    step_x = offset // 9 - 1
    step_y = offset // 3 % 3 - 1
    step_z = offset % 3 - 1
    return (
        ((coord_x + 1 + step_x) * span_y + (coord_y + 1 + step_y)) * span_z
        + (coord_z // M + 1 + step_z) * M
        + within
    )


def update(state, summed, w_message, w_update, gain):
    message = jnp.dot(summed, w_message, preferred_element_type=jnp.float32)
    active = jax.nn.silu(message).astype(jnp.bfloat16)
    residual = state.astype(jnp.float32) + jnp.dot(
        active, w_update, preferred_element_type=jnp.float32
    )
    inv_rms = lax.rsqrt(jnp.mean(residual * residual, axis=-1, keepdims=True) + 1e-06)
    return (residual * inv_rms * gain).astype(jnp.bfloat16)


def shifted(piece, step_x, step_y):
    count_x = lax.axis_size("gx")
    count_y = lax.axis_size("gy")
    pairs = [
        (i * count_y + j, (i + step_x) % count_x * count_y + (j + step_y) % count_y)
        for i in range(count_x)
        for j in range(count_y)
    ]
    return lax.ppermute(piece, ("gx", "gy"), pairs)


def planar_halo(cells):
    head_x, tail_x = cells[:1], cells[-1:]
    low = [
        shifted(tail_x[:, -1:], 1, 1),
        shifted(tail_x, 1, 0),
        shifted(tail_x[:, :1], 1, -1),
    ]
    middle = [shifted(cells[:, -1:], 0, 1), cells, shifted(cells[:, :1], 0, -1)]
    high = [
        shifted(head_x[:, -1:], -1, 1),
        shifted(head_x, -1, 0),
        shifted(head_x[:, :1], -1, -1),
    ]
    return jnp.concatenate(
        [jnp.concatenate(low, axis=1), jnp.concatenate(middle, axis=1), jnp.concatenate(high, axis=1)],
        axis=0,
    )


def ghosts(values):
    deeper = with_halo(values, (("gz", 2),), M, False)
    return planar_halo(deeper)


def candidates(padded, cells_x, cells_y, cells_z):
    feature_width = padded.shape[-1]
    pieces = []
    for step_x in range(3):
        for step_y in range(3):
            for step_z in range(3):
                piece = padded[
                    step_x : step_x + cells_x,
                    step_y : step_y + cells_y,
                    step_z * M : step_z * M + cells_z * M,
                ]
                pieces.append(piece.reshape(cells_x, cells_y, cells_z, M, feature_width))
    stacked = jnp.stack(pieces, axis=3)
    return stacked.reshape(cells_x * cells_y * cells_z, 27 * M, feature_width)


def cheap_layer(state, weights, w_message, w_update, gain):
    cells_x, cells_y, depth, feature_width = state.shape
    cells_z = depth // M
    cell_count = cells_x * cells_y * cells_z
    atom_count = cell_count * M
    nearby = candidates(ghosts(state), cells_x, cells_y, cells_z)
    summed = jnp.einsum(
        "bmkc,bcf->bmkf",
        weights.reshape(cell_count, M, NRB, 27 * M),
        nearby,
        preferred_element_type=jnp.float32,
    )
    summed = summed.reshape(atom_count, NRB * feature_width).astype(jnp.bfloat16)
    return update(
        state.reshape(atom_count, feature_width), summed, w_message, w_update, gain
    ).reshape(state.shape)


def specialist_kernel(env_ref, first_ref, head_ref, out_ref):
    piece = 8
    slots = env_ref.shape[0] // out_ref.shape[0]
    span = piece * slots
    column = lax.broadcasted_iota(jnp.int32, (piece, span), 1)
    row = lax.broadcasted_iota(jnp.int32, (piece, span), 0)
    pool = ((column >= row * slots) & (column < (row + 1) * slots)).astype(jnp.bfloat16)

    def body(index, carry):
        begin = pl.multiple_of(index * span, span)
        message = jnp.dot(
            env_ref[pl.ds(begin, span), :], first_ref[...], preferred_element_type=jnp.float32
        )
        hidden = (message * (0.5 * jnp.tanh(0.5 * message) + 0.5)).astype(jnp.bfloat16)
        pooled = jnp.dot(pool, hidden, preferred_element_type=jnp.float32)
        pooled = (pooled * (1.0 / slots)).astype(jnp.bfloat16)
        out_ref[pl.ds(pl.multiple_of(index * piece, piece), piece), :] = jnp.dot(
            pooled, head_ref[...], preferred_element_type=jnp.float32
        )
        return carry

    lax.fori_loop(0, out_ref.shape[0] // piece, body, 0)


def specialist(received, w_first, w_head):
    sources, item_count, slots, env_width = received.shape
    env_total = sources * item_count
    hidden_width = w_first.shape[-1]
    block = math.gcd(env_total, 32)
    head = jnp.zeros((hidden_width, 128), jnp.bfloat16).at[:, : w_head.shape[0]].set(w_head.T)
    results = pl.pallas_call(
        specialist_kernel,
        grid=(env_total // block,),
        in_specs=[
            pl.BlockSpec((block * slots, env_width), lambda i: (i, 0)),
            pl.BlockSpec((env_width, hidden_width), lambda i: (0, 0)),
            pl.BlockSpec((hidden_width, 128), lambda i: (0, 0)),
        ],
        out_specs=pl.BlockSpec((block, 128), lambda i: (i, 0)),
        out_shape=jax.ShapeDtypeStruct((env_total, 128), jnp.float32),
    )(received.reshape(env_total * slots, env_width), w_first, head)
    return results[:, : w_head.shape[0]].reshape(sources, item_count, w_head.shape[0])


def per_device(
    features,
    neighbour_code,
    distance,
    w_message,
    w_update,
    norm_gain,
    w_env,
    w_out,
    w_first,
    w_head,
    flag_ids,
    flag_owner,
    flag_count,
):
    cells_x, cells_y, depth, feature_width = features.shape
    cells_z = depth // M
    atom_count = cells_x * cells_y * depth
    codes = neighbour_code.reshape(atom_count, -1)
    radial_basis, cutoff = radial(distance.reshape(atom_count, -1))
    code_range = jnp.arange(27 * M, dtype=jnp.int32)
    onehot = (codes[:, :, None] == code_range[None, None, :]).astype(jnp.bfloat16)
    weights = jnp.einsum(
        "ask,asc->akc", radial_basis, onehot, preferred_element_type=jnp.float32
    ).astype(jnp.bfloat16)
    state = features
    for layer_index in range(L):
        state = cheap_layer(
            state,
            weights,
            w_message[layer_index],
            w_update[layer_index],
            norm_gain[layer_index],
        )
    flat_state = state.reshape(atom_count, feature_width)
    projected = jnp.dot(flat_state, w_env, preferred_element_type=jnp.float32).astype(jnp.bfloat16)
    env_width = projected.shape[-1]
    proj_near = candidates(
        ghosts(projected.reshape(cells_x, cells_y, depth, env_width)), cells_x, cells_y, cells_z
    )
    base_force = jnp.einsum("af,cf->ca", flat_state, w_out, preferred_element_type=jnp.float32)
    local_ids = flag_ids.reshape(-1)
    owner = flag_owner.reshape(-1)
    flag_total = local_ids.shape[0]
    live_rows = jnp.arange(flag_total, dtype=jnp.int32) < flag_count.reshape(())
    picked = jnp.einsum(
        "rsc,rce->rse",
        onehot[local_ids],
        proj_near[local_ids // M],
        preferred_element_type=jnp.float32,
    )
    environ = (cutoff[local_ids][..., None] * picked).astype(jnp.bfloat16)
    slots = environ.shape[1]
    owner_total = lax.axis_size("gx") * lax.axis_size("gy")
    capacity = max(2, 2 * flag_total // owner_total)
    same = (owner[:, None] == jnp.arange(owner_total, dtype=jnp.int32)[None, :]).astype(jnp.int32)
    before = jnp.cumsum(same, axis=0) - same
    slot_index = jnp.sum(before * same, axis=1)
    target = jnp.where(live_rows, owner * capacity + slot_index, owner_total * capacity)
    placing = (
        jnp.arange(owner_total * capacity, dtype=jnp.int32)[:, None] == target[None, :]
    ).astype(jnp.bfloat16)
    outgoing = jnp.dot(
        placing, environ.reshape(flag_total, slots * env_width), preferred_element_type=jnp.float32
    ).astype(jnp.bfloat16)
    local_first = w_first[0]
    local_head = w_head[0]
    results = specialist(
        lax.all_to_all(
            outgoing.reshape(owner_total, capacity, slots, env_width),
            ("gx", "gy"),
            split_axis=0,
            concat_axis=0,
            tiled=True,
        ),
        local_first,
        local_head,
    )
    returned = lax.all_to_all(results, ("gx", "gy"), split_axis=0, concat_axis=0, tiled=True)
    returned = returned.reshape(owner_total * capacity, 3)
    correction = returned[jnp.minimum(target, owner_total * capacity - 1)] * live_rows[
        :, None
    ].astype(jnp.float32)
    forces = base_force.at[:, local_ids].add(correction.T)
    return forces.reshape(3, cells_x, cells_y, depth)


def solution(mesh):
    placed = (
        P("gx", "gy", "gz", None),
        P("gx", "gy", "gz", None),
        P("gx", "gy", "gz", None),
        P(),
        P(),
        P(),
        P(),
        P(),
        P(("gx", "gy"), None, None),
        P(("gx", "gy"), None, None),
        P("gx", "gy", "gz", None),
        P("gx", "gy", "gz", None, None),
        P("gx", "gy", "gz"),
    )
    return jax.shard_map(
        per_device, mesh=mesh, in_specs=placed, out_specs=P(None, "gx", "gy", "gz"), check_vma=False
    )
```

```python
import math

import jax
import jax.numpy as jnp
from jax import lax
from jax.sharding import PartitionSpec as P
from jax.experimental import pallas as pl

M = 4
NRB = 8
L = 2


CUTOFF_RADIUS = 5.0
WIDTH_GAMMA = 2.0


def with_halo(cells, sides, width, closed):
    for axis, dim in sides:
        count = lax.axis_size(axis)
        ends = count if closed else count - 1
        head = lax.slice_in_dim(cells, 0, width, axis=dim)
        tail = lax.slice_in_dim(cells, cells.shape[dim] - width, cells.shape[dim], axis=dim)
        cells = jnp.concatenate(
            [
                lax.ppermute(tail, axis, [(i, (i + 1) % count) for i in range(ends)]),
                cells,
                lax.ppermute(head, axis, [((i + 1) % count, i) for i in range(ends)]),
            ],
            axis=dim,
        )
    return cells


def radial(distance):
    cutoff = 0.5 * (jnp.cos(jnp.pi * distance / CUTOFF_RADIUS) + 1.0)
    centres = 0.8 + jnp.arange(NRB).astype(distance.dtype) * (4.0 / (NRB - 1))
    radial_basis = jnp.exp(-WIDTH_GAMMA * (distance[..., None] - centres) ** 2) * cutoff[..., None]
    return (radial_basis.astype(jnp.bfloat16), cutoff)


def neighbour_rows(codes, coord_x, coord_y, coord_z, span_y, span_z):
    offset = codes // M
    within = codes % M
    step_x = offset // 9 - 1
    step_y = offset // 3 % 3 - 1
    step_z = offset % 3 - 1
    return (
        ((coord_x + 1 + step_x) * span_y + (coord_y + 1 + step_y)) * span_z
        + (coord_z // M + 1 + step_z) * M
        + within
    )


def update(state, summed, w_message, w_update, gain):
    message = jnp.dot(summed, w_message, preferred_element_type=jnp.float32)
    active = jax.nn.silu(message).astype(jnp.bfloat16)
    residual = state.astype(jnp.float32) + jnp.dot(
        active, w_update, preferred_element_type=jnp.float32
    )
    inv_rms = lax.rsqrt(jnp.mean(residual * residual, axis=-1, keepdims=True) + 1e-06)
    return (residual * inv_rms * gain).astype(jnp.bfloat16)


def ghosts(values):
    deeper = with_halo(values, (("gz", 2),), M, False)
    return with_halo(deeper, (("gx", 0), ("gy", 1)), 1, True)


def candidates(padded, cells_x, cells_y, cells_z):
    feature_width = padded.shape[-1]
    pieces = []
    for step_x in range(3):
        for step_y in range(3):
            for step_z in range(3):
                piece = padded[
                    step_x : step_x + cells_x,
                    step_y : step_y + cells_y,
                    step_z * M : step_z * M + cells_z * M,
                ]
                pieces.append(piece.reshape(cells_x, cells_y, cells_z, M, feature_width))
    stacked = jnp.stack(pieces, axis=3)
    return stacked.reshape(cells_x * cells_y * cells_z, 27 * M, feature_width)


def cheap_layer(state, weights, w_message, w_update, gain):
    cells_x, cells_y, depth, feature_width = state.shape
    cells_z = depth // M
    cell_count = cells_x * cells_y * cells_z
    atom_count = cell_count * M
    nearby = candidates(ghosts(state), cells_x, cells_y, cells_z)
    summed = jnp.einsum(
        "bmkc,bcf->bmkf",
        weights.reshape(cell_count, M, NRB, 27 * M),
        nearby,
        preferred_element_type=jnp.float32,
    )
    summed = summed.reshape(atom_count, NRB * feature_width).astype(jnp.bfloat16)
    return update(
        state.reshape(atom_count, feature_width), summed, w_message, w_update, gain
    ).reshape(state.shape)


def specialist_kernel(env_ref, first_ref, head_ref, out_ref):
    piece = 64
    slots = env_ref.shape[0] // out_ref.shape[0]
    span = piece * slots
    column = lax.broadcasted_iota(jnp.int32, (piece, span), 1)
    row = lax.broadcasted_iota(jnp.int32, (piece, span), 0)
    pool = ((column >= row * slots) & (column < (row + 1) * slots)).astype(jnp.bfloat16)

    def body(index, carry):
        begin = pl.multiple_of(index * span, span)
        message = jnp.dot(
            env_ref[pl.ds(begin, span), :], first_ref[...], preferred_element_type=jnp.float32
        )
        hidden = jax.nn.silu(message).astype(jnp.bfloat16)
        pooled = jnp.dot(pool, hidden, preferred_element_type=jnp.float32)
        pooled = (pooled * (1.0 / slots)).astype(jnp.bfloat16)
        out_ref[pl.ds(pl.multiple_of(index * piece, piece), piece), :] = jnp.dot(
            pooled, head_ref[...], preferred_element_type=jnp.float32
        )
        return carry

    lax.fori_loop(0, out_ref.shape[0] // piece, body, 0)


def specialist(received, w_first, w_head):
    sources, item_count, slots, env_width = received.shape
    env_total = sources * item_count
    hidden_width = w_first.shape[-1]
    block = math.gcd(env_total, 64)
    head = jnp.zeros((hidden_width, 128), jnp.bfloat16).at[:, : w_head.shape[0]].set(w_head.T)
    results = pl.pallas_call(
        specialist_kernel,
        grid=(env_total // block,),
        in_specs=[
            pl.BlockSpec((block * slots, env_width), lambda i: (i, 0)),
            pl.BlockSpec((env_width, hidden_width), lambda i: (0, 0)),
            pl.BlockSpec((hidden_width, 128), lambda i: (0, 0)),
        ],
        out_specs=pl.BlockSpec((block, 128), lambda i: (i, 0)),
        out_shape=jax.ShapeDtypeStruct((env_total, 128), jnp.float32),
    )(received.reshape(env_total * slots, env_width), w_first, head)
    return results[:, : w_head.shape[0]].reshape(sources, item_count, w_head.shape[0])


def per_device(
    features,
    neighbour_code,
    distance,
    w_message,
    w_update,
    norm_gain,
    w_env,
    w_out,
    w_first,
    w_head,
    flag_ids,
    flag_owner,
    flag_count,
):
    cells_x, cells_y, depth, feature_width = features.shape
    cells_z = depth // M
    atom_count = cells_x * cells_y * depth
    codes = neighbour_code.reshape(atom_count, -1)
    radial_basis, cutoff = radial(distance.reshape(atom_count, -1))
    code_range = jnp.arange(27 * M, dtype=jnp.int32)
    onehot = (codes[:, :, None] == code_range[None, None, :]).astype(jnp.bfloat16)
    weights = jnp.einsum(
        "ask,asc->akc", radial_basis, onehot, preferred_element_type=jnp.float32
    ).astype(jnp.bfloat16)
    state = features
    for layer_index in range(L):
        state = cheap_layer(
            state,
            weights,
            w_message[layer_index],
            w_update[layer_index],
            norm_gain[layer_index],
        )
    flat_state = state.reshape(atom_count, feature_width)
    projected = jnp.dot(flat_state, w_env, preferred_element_type=jnp.float32).astype(jnp.bfloat16)
    env_width = projected.shape[-1]
    proj_near = candidates(
        ghosts(projected.reshape(cells_x, cells_y, depth, env_width)), cells_x, cells_y, cells_z
    )
    base_force = jnp.einsum("af,cf->ca", flat_state, w_out, preferred_element_type=jnp.float32)
    local_ids = flag_ids.reshape(-1)
    owner = flag_owner.reshape(-1)
    flag_total = local_ids.shape[0]
    live_rows = jnp.arange(flag_total, dtype=jnp.int32) < flag_count.reshape(())
    picked = jnp.einsum(
        "rsc,rce->rse",
        onehot[local_ids],
        proj_near[local_ids // M],
        preferred_element_type=jnp.float32,
    )
    environ = (cutoff[local_ids][..., None] * picked).astype(jnp.bfloat16)
    slots = environ.shape[1]
    owner_total = lax.axis_size("gx") * lax.axis_size("gy")
    capacity = max(2, 2 * flag_total // owner_total)
    same = (owner[:, None] == jnp.arange(owner_total, dtype=jnp.int32)[None, :]).astype(jnp.int32)
    before = jnp.cumsum(same, axis=0) - same
    slot_index = jnp.sum(before * same, axis=1)
    target = jnp.where(live_rows, owner * capacity + slot_index, owner_total * capacity)
    placing = (
        jnp.arange(owner_total * capacity, dtype=jnp.int32)[:, None] == target[None, :]
    ).astype(jnp.bfloat16)
    outgoing = jnp.dot(
        placing, environ.reshape(flag_total, slots * env_width), preferred_element_type=jnp.float32
    ).astype(jnp.bfloat16)
    local_first = w_first[0]
    local_head = w_head[0]
    results = specialist(
        lax.all_to_all(
            outgoing.reshape(owner_total, capacity, slots, env_width),
            ("gx", "gy"),
            split_axis=0,
            concat_axis=0,
            tiled=True,
        ),
        local_first,
        local_head,
    )
    returned = lax.all_to_all(results, ("gx", "gy"), split_axis=0, concat_axis=0, tiled=True)
    returned = returned.reshape(owner_total * capacity, 3)
    correction = returned[jnp.minimum(target, owner_total * capacity - 1)] * live_rows[
        :, None
    ].astype(jnp.float32)
    forces = base_force.at[:, local_ids].add(correction.T)
    return forces.reshape(3, cells_x, cells_y, depth)


def solution(mesh):
    placed = (
        P("gx", "gy", "gz", None),
        P("gx", "gy", "gz", None),
        P("gx", "gy", "gz", None),
        P(),
        P(),
        P(),
        P(),
        P(),
        P(("gx", "gy"), None, None),
        P(("gx", "gy"), None, None),
        P("gx", "gy", "gz", None),
        P("gx", "gy", "gz", None, None),
        P("gx", "gy", "gz"),
    )
    return jax.shard_map(
        per_device, mesh=mesh, in_specs=placed, out_specs=P(None, "gx", "gy", "gz"), check_vma=False
    )
```

```python
import math

import jax
import jax.numpy as jnp
from jax import lax
from jax.sharding import PartitionSpec as P
from jax.experimental import pallas as pl

M = 4
NRB = 8
L = 2


CUTOFF_RADIUS = 5.0
WIDTH_GAMMA = 2.0


def with_halo(cells, sides, width, closed):
    for axis, dim in sides:
        count = lax.axis_size(axis)
        ends = count if closed else count - 1
        head = lax.slice_in_dim(cells, 0, width, axis=dim)
        tail = lax.slice_in_dim(cells, cells.shape[dim] - width, cells.shape[dim], axis=dim)
        cells = jnp.concatenate(
            [
                lax.ppermute(tail, axis, [(i, (i + 1) % count) for i in range(ends)]),
                cells,
                lax.ppermute(head, axis, [((i + 1) % count, i) for i in range(ends)]),
            ],
            axis=dim,
        )
    return cells


def radial(distance):
    cutoff = 0.5 * (jnp.cos(jnp.pi * distance / CUTOFF_RADIUS) + 1.0)
    centres = 0.8 + jnp.arange(NRB).astype(distance.dtype) * (4.0 / (NRB - 1))
    radial_basis = jnp.exp(-WIDTH_GAMMA * (distance[..., None] - centres) ** 2) * cutoff[..., None]
    return (radial_basis.astype(jnp.bfloat16), cutoff)


def neighbour_rows(codes, coord_x, coord_y, coord_z, span_y, span_z):
    offset = codes // M
    within = codes % M
    step_x = offset // 9 - 1
    step_y = offset // 3 % 3 - 1
    step_z = offset % 3 - 1
    return (
        ((coord_x + 1 + step_x) * span_y + (coord_y + 1 + step_y)) * span_z
        + (coord_z // M + 1 + step_z) * M
        + within
    )


def update(state, summed, w_message, w_update, gain):
    message = jnp.dot(summed, w_message, preferred_element_type=jnp.float32)
    active = jax.nn.silu(message).astype(jnp.bfloat16)
    residual = state.astype(jnp.float32) + jnp.dot(
        active, w_update, preferred_element_type=jnp.float32
    )
    inv_rms = lax.rsqrt(jnp.mean(residual * residual, axis=-1, keepdims=True) + 1e-06)
    return (residual * inv_rms * gain).astype(jnp.bfloat16)


def ghosts(values):
    wider = with_halo(values, (("gx", 0), ("gy", 1)), 1, True)
    return with_halo(wider, (("gz", 2),), M, False)


def candidates(padded, cells_x, cells_y, cells_z):
    feature_width = padded.shape[-1]
    pieces = []
    for step_x in range(3):
        for step_y in range(3):
            for step_z in range(3):
                piece = padded[
                    step_x : step_x + cells_x,
                    step_y : step_y + cells_y,
                    step_z * M : step_z * M + cells_z * M,
                ]
                pieces.append(piece.reshape(cells_x, cells_y, cells_z, M, feature_width))
    stacked = jnp.stack(pieces, axis=3)
    return stacked.reshape(cells_x * cells_y * cells_z, 27 * M, feature_width)


def cheap_layer(state, weights, w_message, w_update, gain):
    cells_x, cells_y, depth, feature_width = state.shape
    cells_z = depth // M
    cell_count = cells_x * cells_y * cells_z
    atom_count = cell_count * M
    nearby = candidates(ghosts(state), cells_x, cells_y, cells_z)
    summed = jnp.einsum(
        "bmkc,bcf->bmkf",
        weights.reshape(cell_count, M, NRB, 27 * M),
        nearby,
        preferred_element_type=jnp.float32,
    )
    summed = summed.reshape(atom_count, NRB * feature_width).astype(jnp.bfloat16)
    return update(
        state.reshape(atom_count, feature_width), summed, w_message, w_update, gain
    ).reshape(state.shape)


def specialist_kernel(env_ref, first_ref, head_ref, out_ref):
    piece = 64
    slots = env_ref.shape[0] // out_ref.shape[0]
    span = piece * slots
    column = lax.broadcasted_iota(jnp.int32, (piece, span), 1)
    row = lax.broadcasted_iota(jnp.int32, (piece, span), 0)
    pool = ((column >= row * slots) & (column < (row + 1) * slots)).astype(jnp.bfloat16)

    def body(index, carry):
        begin = pl.multiple_of(index * span, span)
        message = jnp.dot(
            env_ref[pl.ds(begin, span), :], first_ref[...], preferred_element_type=jnp.float32
        )
        hidden = jax.nn.silu(message).astype(jnp.bfloat16)
        pooled = jnp.dot(pool, hidden, preferred_element_type=jnp.float32)
        pooled = (pooled * (1.0 / slots)).astype(jnp.bfloat16)
        out_ref[pl.ds(pl.multiple_of(index * piece, piece), piece), :] = jnp.dot(
            pooled, head_ref[...], preferred_element_type=jnp.float32
        )
        return carry

    lax.fori_loop(0, out_ref.shape[0] // piece, body, 0)


def specialist(received, w_first, w_head):
    sources, item_count, slots, env_width = received.shape
    env_total = sources * item_count
    hidden_width = w_first.shape[-1]
    block = math.gcd(env_total, 64)
    head = jnp.zeros((hidden_width, 128), jnp.bfloat16).at[:, : w_head.shape[0]].set(w_head.T)
    results = pl.pallas_call(
        specialist_kernel,
        grid=(env_total // block,),
        in_specs=[
            pl.BlockSpec((block * slots, env_width), lambda i: (i, 0)),
            pl.BlockSpec((env_width, hidden_width), lambda i: (0, 0)),
            pl.BlockSpec((hidden_width, 128), lambda i: (0, 0)),
        ],
        out_specs=pl.BlockSpec((block, 128), lambda i: (i, 0)),
        out_shape=jax.ShapeDtypeStruct((env_total, 128), jnp.float32),
    )(received.reshape(env_total * slots, env_width), w_first, head)
    return results[:, : w_head.shape[0]].reshape(sources, item_count, w_head.shape[0])


def per_device(
    features,
    neighbour_code,
    distance,
    w_message,
    w_update,
    norm_gain,
    w_env,
    w_out,
    w_first,
    w_head,
    flag_ids,
    flag_owner,
    flag_count,
):
    cells_x, cells_y, depth, feature_width = features.shape
    cells_z = depth // M
    atom_count = cells_x * cells_y * depth
    codes = neighbour_code.reshape(atom_count, -1)
    radial_basis, cutoff = radial(distance.reshape(atom_count, -1))
    code_range = jnp.arange(27 * M, dtype=jnp.int32)
    onehot = (codes[:, :, None] == code_range[None, None, :]).astype(jnp.bfloat16)
    weights = jnp.einsum(
        "ask,asc->akc", radial_basis, onehot, preferred_element_type=jnp.float32
    ).astype(jnp.bfloat16)
    state = features
    for layer_index in range(L):
        state = cheap_layer(
            state,
            weights,
            w_message[layer_index],
            w_update[layer_index],
            norm_gain[layer_index],
        )
    flat_state = state.reshape(atom_count, feature_width)
    projected = jnp.dot(flat_state, w_env, preferred_element_type=jnp.float32).astype(jnp.bfloat16)
    env_width = projected.shape[-1]
    proj_near = candidates(
        ghosts(projected.reshape(cells_x, cells_y, depth, env_width)), cells_x, cells_y, cells_z
    )
    base_force = jnp.einsum("af,cf->ca", flat_state, w_out, preferred_element_type=jnp.float32)
    local_ids = flag_ids.reshape(-1)
    owner = flag_owner.reshape(-1)
    flag_total = local_ids.shape[0]
    live_rows = jnp.arange(flag_total, dtype=jnp.int32) < flag_count.reshape(())
    picked = jnp.einsum(
        "rsc,rce->rse",
        onehot[local_ids],
        proj_near[local_ids // M],
        preferred_element_type=jnp.float32,
    )
    environ = (cutoff[local_ids][..., None] * picked).astype(jnp.bfloat16)
    slots = environ.shape[1]
    owner_total = lax.axis_size("gx") * lax.axis_size("gy")
    capacity = max(2, 2 * flag_total // owner_total)
    same = (owner[:, None] == jnp.arange(owner_total, dtype=jnp.int32)[None, :]).astype(jnp.int32)
    before = jnp.cumsum(same, axis=0) - same
    slot_index = jnp.sum(before * same, axis=1)
    target = jnp.where(live_rows, owner * capacity + slot_index, owner_total * capacity)
    placing = (
        jnp.arange(owner_total * capacity, dtype=jnp.int32)[:, None] == target[None, :]
    ).astype(jnp.bfloat16)
    outgoing = jnp.dot(
        placing, environ.reshape(flag_total, slots * env_width), preferred_element_type=jnp.float32
    ).astype(jnp.bfloat16)
    local_first = w_first[0]
    local_head = w_head[0]
    results = specialist(
        lax.all_to_all(
            outgoing.reshape(owner_total, capacity, slots, env_width),
            ("gx", "gy"),
            split_axis=0,
            concat_axis=0,
            tiled=True,
        ),
        local_first,
        local_head,
    )
    returned = lax.all_to_all(results, ("gx", "gy"), split_axis=0, concat_axis=0, tiled=True)
    returned = returned.reshape(owner_total * capacity, 3)
    correction = returned[jnp.minimum(target, owner_total * capacity - 1)] * live_rows[
        :, None
    ].astype(jnp.float32)
    forces = base_force.at[:, local_ids].add(correction.T)
    return forces.reshape(3, cells_x, cells_y, depth)


def solution(mesh):
    placed = (
        P("gx", "gy", "gz", None),
        P("gx", "gy", "gz", None),
        P("gx", "gy", "gz", None),
        P(),
        P(),
        P(),
        P(),
        P(),
        P(("gx", "gy"), None, None),
        P(("gx", "gy"), None, None),
        P("gx", "gy", "gz", None),
        P("gx", "gy", "gz", None, None),
        P("gx", "gy", "gz"),
    )
    return jax.shard_map(
        per_device, mesh=mesh, in_specs=placed, out_specs=P(None, "gx", "gy", "gz"), check_vma=False
    )
```

```python
import math

import jax
import jax.numpy as jnp
from jax import lax
from jax.sharding import PartitionSpec as P
from jax.experimental import pallas as pl

M = 4
NRB = 8
L = 2


CUTOFF_RADIUS = 5.0
WIDTH_GAMMA = 2.0


def with_halo(cells, sides, width, closed):
    for axis, dim in sides:
        count = lax.axis_size(axis)
        ends = count if closed else count - 1
        head = lax.slice_in_dim(cells, 0, width, axis=dim)
        tail = lax.slice_in_dim(cells, cells.shape[dim] - width, cells.shape[dim], axis=dim)
        cells = jnp.concatenate(
            [
                lax.ppermute(tail, axis, [(i, (i + 1) % count) for i in range(ends)]),
                cells,
                lax.ppermute(head, axis, [((i + 1) % count, i) for i in range(ends)]),
            ],
            axis=dim,
        )
    return cells


def radial(distance):
    cutoff = 0.5 * (jnp.cos(jnp.pi * distance / CUTOFF_RADIUS) + 1.0)
    centres = 0.8 + jnp.arange(NRB).astype(distance.dtype) * (4.0 / (NRB - 1))
    radial_basis = jnp.exp(-WIDTH_GAMMA * (distance[..., None] - centres) ** 2) * cutoff[..., None]
    return (radial_basis.astype(jnp.bfloat16), cutoff)


def neighbour_rows(codes, coord_x, coord_y, coord_z, span_y, span_z):
    offset = codes // M
    within = codes % M
    step_x = offset // 9 - 1
    step_y = offset // 3 % 3 - 1
    step_z = offset % 3 - 1
    return (
        ((coord_x + 1 + step_x) * span_y + (coord_y + 1 + step_y)) * span_z
        + (coord_z // M + 1 + step_z) * M
        + within
    )


def update(state, summed, w_message, w_update, gain):
    message = jnp.dot(summed, w_message, preferred_element_type=jnp.float32)
    active = jax.nn.silu(message).astype(jnp.bfloat16)
    residual = state.astype(jnp.float32) + jnp.dot(
        active, w_update, preferred_element_type=jnp.float32
    )
    inv_rms = lax.rsqrt(jnp.mean(residual * residual, axis=-1, keepdims=True) + 1e-06)
    return (residual * inv_rms * gain).astype(jnp.bfloat16)


def ghosts(values):
    wider = with_halo(values, (("gy", 1), ("gx", 0)), 1, True)
    return with_halo(wider, (("gz", 2),), M, False)


def candidates(padded, cells_x, cells_y, cells_z):
    feature_width = padded.shape[-1]
    pieces = []
    for step_x in range(3):
        for step_y in range(3):
            for step_z in range(3):
                piece = padded[
                    step_x : step_x + cells_x,
                    step_y : step_y + cells_y,
                    step_z * M : step_z * M + cells_z * M,
                ]
                pieces.append(piece.reshape(cells_x, cells_y, cells_z, M, feature_width))
    stacked = jnp.stack(pieces, axis=3)
    return stacked.reshape(cells_x * cells_y * cells_z, 27 * M, feature_width)


def cheap_layer(state, weights, w_message, w_update, gain):
    cells_x, cells_y, depth, feature_width = state.shape
    cells_z = depth // M
    cell_count = cells_x * cells_y * cells_z
    atom_count = cell_count * M
    nearby = candidates(ghosts(state), cells_x, cells_y, cells_z)
    summed = jnp.einsum(
        "bmkc,bcf->bmkf",
        weights.reshape(cell_count, M, NRB, 27 * M),
        nearby,
        preferred_element_type=jnp.float32,
    )
    summed = summed.reshape(atom_count, NRB * feature_width).astype(jnp.bfloat16)
    return update(
        state.reshape(atom_count, feature_width), summed, w_message, w_update, gain
    ).reshape(state.shape)


def specialist_kernel(env_ref, first_ref, head_ref, out_ref):
    piece = 64
    slots = env_ref.shape[0] // out_ref.shape[0]
    span = piece * slots
    column = lax.broadcasted_iota(jnp.int32, (piece, span), 1)
    row = lax.broadcasted_iota(jnp.int32, (piece, span), 0)
    pool = ((column >= row * slots) & (column < (row + 1) * slots)).astype(jnp.bfloat16)

    def body(index, carry):
        begin = pl.multiple_of(index * span, span)
        message = jnp.dot(
            env_ref[pl.ds(begin, span), :], first_ref[...], preferred_element_type=jnp.float32
        )
        hidden = jax.nn.silu(message).astype(jnp.bfloat16)
        pooled = jnp.dot(pool, hidden, preferred_element_type=jnp.float32)
        pooled = (pooled * (1.0 / slots)).astype(jnp.bfloat16)
        out_ref[pl.ds(pl.multiple_of(index * piece, piece), piece), :] = jnp.dot(
            pooled, head_ref[...], preferred_element_type=jnp.float32
        )
        return carry

    lax.fori_loop(0, out_ref.shape[0] // piece, body, 0)


def specialist(received, w_first, w_head):
    sources, item_count, slots, env_width = received.shape
    env_total = sources * item_count
    hidden_width = w_first.shape[-1]
    block = math.gcd(env_total, 64)
    head = jnp.zeros((hidden_width, 128), jnp.bfloat16).at[:, : w_head.shape[0]].set(w_head.T)
    results = pl.pallas_call(
        specialist_kernel,
        grid=(env_total // block,),
        in_specs=[
            pl.BlockSpec((block * slots, env_width), lambda i: (i, 0)),
            pl.BlockSpec((env_width, hidden_width), lambda i: (0, 0)),
            pl.BlockSpec((hidden_width, 128), lambda i: (0, 0)),
        ],
        out_specs=pl.BlockSpec((block, 128), lambda i: (i, 0)),
        out_shape=jax.ShapeDtypeStruct((env_total, 128), jnp.float32),
    )(received.reshape(env_total * slots, env_width), w_first, head)
    return results[:, : w_head.shape[0]].reshape(sources, item_count, w_head.shape[0])


def per_device(
    features,
    neighbour_code,
    distance,
    w_message,
    w_update,
    norm_gain,
    w_env,
    w_out,
    w_first,
    w_head,
    flag_ids,
    flag_owner,
    flag_count,
):
    cells_x, cells_y, depth, feature_width = features.shape
    cells_z = depth // M
    atom_count = cells_x * cells_y * depth
    codes = neighbour_code.reshape(atom_count, -1)
    radial_basis, cutoff = radial(distance.reshape(atom_count, -1))
    code_range = jnp.arange(27 * M, dtype=jnp.int32)
    onehot = (codes[:, :, None] == code_range[None, None, :]).astype(jnp.bfloat16)
    weights = jnp.einsum(
        "ask,asc->akc", radial_basis, onehot, preferred_element_type=jnp.float32
    ).astype(jnp.bfloat16)
    state = features
    for layer_index in range(L):
        state = cheap_layer(
            state,
            weights,
            w_message[layer_index],
            w_update[layer_index],
            norm_gain[layer_index],
        )
    flat_state = state.reshape(atom_count, feature_width)
    projected = jnp.dot(flat_state, w_env, preferred_element_type=jnp.float32).astype(jnp.bfloat16)
    env_width = projected.shape[-1]
    proj_near = candidates(
        ghosts(projected.reshape(cells_x, cells_y, depth, env_width)), cells_x, cells_y, cells_z
    )
    base_force = jnp.einsum("af,cf->ca", flat_state, w_out, preferred_element_type=jnp.float32)
    local_ids = flag_ids.reshape(-1)
    owner = flag_owner.reshape(-1)
    flag_total = local_ids.shape[0]
    live_rows = jnp.arange(flag_total, dtype=jnp.int32) < flag_count.reshape(())
    picked = jnp.einsum(
        "rsc,rce->rse",
        onehot[local_ids],
        proj_near[local_ids // M],
        preferred_element_type=jnp.float32,
    )
    environ = (cutoff[local_ids][..., None] * picked).astype(jnp.bfloat16)
    slots = environ.shape[1]
    owner_total = lax.axis_size("gx") * lax.axis_size("gy")
    capacity = max(2, 2 * flag_total // owner_total)
    same = (owner[:, None] == jnp.arange(owner_total, dtype=jnp.int32)[None, :]).astype(jnp.int32)
    before = jnp.cumsum(same, axis=0) - same
    slot_index = jnp.sum(before * same, axis=1)
    target = jnp.where(live_rows, owner * capacity + slot_index, owner_total * capacity)
    placing = (
        jnp.arange(owner_total * capacity, dtype=jnp.int32)[:, None] == target[None, :]
    ).astype(jnp.bfloat16)
    outgoing = jnp.dot(
        placing, environ.reshape(flag_total, slots * env_width), preferred_element_type=jnp.float32
    ).astype(jnp.bfloat16)
    local_first = w_first[0]
    local_head = w_head[0]
    results = specialist(
        lax.all_to_all(
            outgoing.reshape(owner_total, capacity, slots, env_width),
            ("gx", "gy"),
            split_axis=0,
            concat_axis=0,
            tiled=True,
        ),
        local_first,
        local_head,
    )
    returned = lax.all_to_all(results, ("gx", "gy"), split_axis=0, concat_axis=0, tiled=True)
    returned = returned.reshape(owner_total * capacity, 3)
    correction = returned[jnp.minimum(target, owner_total * capacity - 1)] * live_rows[
        :, None
    ].astype(jnp.float32)
    forces = base_force.at[:, local_ids].add(correction.T)
    return forces.reshape(3, cells_x, cells_y, depth)


def solution(mesh):
    placed = (
        P("gx", "gy", "gz", None),
        P("gx", "gy", "gz", None),
        P("gx", "gy", "gz", None),
        P(),
        P(),
        P(),
        P(),
        P(),
        P(("gx", "gy"), None, None),
        P(("gx", "gy"), None, None),
        P("gx", "gy", "gz", None),
        P("gx", "gy", "gz", None, None),
        P("gx", "gy", "gz"),
    )
    return jax.shard_map(
        per_device, mesh=mesh, in_specs=placed, out_specs=P(None, "gx", "gy", "gz"), check_vma=False
    )
```

```python
import math

import jax
import jax.numpy as jnp
from jax import lax
from jax.sharding import PartitionSpec as P
from jax.experimental import pallas as pl

M = 4
NRB = 8
L = 2


CUTOFF_RADIUS = 5.0
WIDTH_GAMMA = 2.0


def with_halo(cells, sides, width, closed):
    for axis, dim in sides:
        count = lax.axis_size(axis)
        ends = count if closed else count - 1
        head = lax.slice_in_dim(cells, 0, width, axis=dim)
        tail = lax.slice_in_dim(cells, cells.shape[dim] - width, cells.shape[dim], axis=dim)
        cells = jnp.concatenate(
            [
                lax.ppermute(tail, axis, [(i, (i + 1) % count) for i in range(ends)]),
                cells,
                lax.ppermute(head, axis, [((i + 1) % count, i) for i in range(ends)]),
            ],
            axis=dim,
        )
    return cells


def radial(distance):
    cutoff = 0.5 * (jnp.cos(jnp.pi * distance / CUTOFF_RADIUS) + 1.0)
    centres = 0.8 + jnp.arange(NRB).astype(distance.dtype) * (4.0 / (NRB - 1))
    radial_basis = jnp.exp(-WIDTH_GAMMA * (distance[..., None] - centres) ** 2) * cutoff[..., None]
    return (radial_basis.astype(jnp.bfloat16), cutoff)


def neighbour_rows(codes, coord_x, coord_y, coord_z, span_y, span_z):
    offset = codes // M
    within = codes % M
    step_x = offset // 9 - 1
    step_y = offset // 3 % 3 - 1
    step_z = offset % 3 - 1
    return (
        ((coord_x + 1 + step_x) * span_y + (coord_y + 1 + step_y)) * span_z
        + (coord_z // M + 1 + step_z) * M
        + within
    )


def update(state, summed, w_message, w_update, gain):
    message = jnp.dot(summed, w_message, preferred_element_type=jnp.float32)
    active = jax.nn.silu(message).astype(jnp.bfloat16)
    residual = state.astype(jnp.float32) + jnp.dot(
        active, w_update, preferred_element_type=jnp.float32
    )
    inv_rms = lax.rsqrt(jnp.mean(residual * residual, axis=-1, keepdims=True) + 1e-06)
    return (residual * inv_rms * gain).astype(jnp.bfloat16)


def ghosts(values):
    wider = with_halo(values, (("gy", 1), ("gx", 0)), 1, True)
    return with_halo(wider, (("gz", 2),), M, False)


def candidates(padded, cells_x, cells_y, cells_z):
    feature_width = padded.shape[-1]
    pieces = []
    for step_x in range(3):
        for step_y in range(3):
            for step_z in range(3):
                piece = padded[
                    step_x : step_x + cells_x,
                    step_y : step_y + cells_y,
                    step_z * M : step_z * M + cells_z * M,
                ]
                pieces.append(piece.reshape(cells_x, cells_y, cells_z, M, feature_width))
    stacked = jnp.stack(pieces, axis=3)
    return stacked.reshape(cells_x * cells_y * cells_z, 27 * M, feature_width)


def cheap_layer(state, weights, w_message, w_update, gain):
    cells_x, cells_y, depth, feature_width = state.shape
    cells_z = depth // M
    cell_count = cells_x * cells_y * cells_z
    atom_count = cell_count * M
    nearby = candidates(ghosts(state), cells_x, cells_y, cells_z)
    summed = jnp.einsum(
        "bmkc,bcf->bmkf",
        weights.reshape(cell_count, M, NRB, 27 * M),
        nearby,
        preferred_element_type=jnp.float32,
    )
    summed = summed.reshape(atom_count, NRB * feature_width).astype(jnp.bfloat16)
    return update(
        state.reshape(atom_count, feature_width), summed, w_message, w_update, gain
    ).reshape(state.shape)


def specialist_kernel(env_ref, first_ref, head_ref, out_ref):
    piece = 64
    slots = env_ref.shape[0] // out_ref.shape[0]
    span = piece * slots
    column = lax.broadcasted_iota(jnp.int32, (piece, span), 1)
    row = lax.broadcasted_iota(jnp.int32, (piece, span), 0)
    pool = ((column >= row * slots) & (column < (row + 1) * slots)).astype(jnp.bfloat16)

    def body(index, carry):
        begin = pl.multiple_of(index * span, span)
        message = jnp.dot(
            env_ref[pl.ds(begin, span), :], first_ref[...], preferred_element_type=jnp.float32
        )
        hidden = jax.nn.silu(message).astype(jnp.bfloat16)
        pooled = jnp.dot(pool, hidden, preferred_element_type=jnp.float32)
        pooled = (pooled * (1.0 / slots)).astype(jnp.bfloat16)
        out_ref[pl.ds(pl.multiple_of(index * piece, piece), piece), :] = jnp.dot(
            pooled, head_ref[...], preferred_element_type=jnp.float32
        )
        return carry

    lax.fori_loop(0, out_ref.shape[0] // piece, body, 0)


def specialist(received, w_first, w_head):
    sources, item_count, slots, env_width = received.shape
    env_total = sources * item_count
    hidden_width = w_first.shape[-1]
    block = math.gcd(env_total, 64)
    head = jnp.zeros((hidden_width, 128), jnp.bfloat16).at[:, : w_head.shape[0]].set(w_head.T)
    results = pl.pallas_call(
        specialist_kernel,
        grid=(env_total // block,),
        in_specs=[
            pl.BlockSpec((block * slots, env_width), lambda i: (i, 0)),
            pl.BlockSpec((env_width, hidden_width), lambda i: (0, 0)),
            pl.BlockSpec((hidden_width, 128), lambda i: (0, 0)),
        ],
        out_specs=pl.BlockSpec((block, 128), lambda i: (i, 0)),
        out_shape=jax.ShapeDtypeStruct((env_total, 128), jnp.float32),
    )(received.reshape(env_total * slots, env_width), w_first, head)
    return results[:, : w_head.shape[0]].reshape(sources, item_count, w_head.shape[0])


def per_device(
    features,
    neighbour_code,
    distance,
    w_message,
    w_update,
    norm_gain,
    w_env,
    w_out,
    w_first,
    w_head,
    flag_ids,
    flag_owner,
    flag_count,
):
    cells_x, cells_y, depth, feature_width = features.shape
    cells_z = depth // M
    atom_count = cells_x * cells_y * depth
    codes = neighbour_code.reshape(atom_count, -1)
    radial_basis, cutoff = radial(distance.reshape(atom_count, -1))
    code_range = jnp.arange(27 * M, dtype=jnp.int32)
    onehot = (codes[:, :, None] == code_range[None, None, :]).astype(jnp.bfloat16)
    weights = jnp.einsum(
        "ask,asc->akc", radial_basis, onehot, preferred_element_type=jnp.float32
    ).astype(jnp.bfloat16)
    state = features
    for layer_index in range(L):
        state = cheap_layer(
            state,
            weights,
            w_message[layer_index],
            w_update[layer_index],
            norm_gain[layer_index],
        )
    flat_state = state.reshape(atom_count, feature_width)
    projected = jnp.dot(flat_state, w_env, preferred_element_type=jnp.float32).astype(jnp.bfloat16)
    env_width = projected.shape[-1]
    proj_near = candidates(
        ghosts(projected.reshape(cells_x, cells_y, depth, env_width)), cells_x, cells_y, cells_z
    )
    base_force = jnp.einsum("af,cf->ca", flat_state, w_out, preferred_element_type=jnp.float32)
    local_ids = flag_ids.reshape(-1)
    owner = flag_owner.reshape(-1)
    flag_total = local_ids.shape[0]
    live_rows = jnp.arange(flag_total, dtype=jnp.int32) < flag_count.reshape(())
    picked = jnp.einsum(
        "rsc,rce->rse",
        onehot[local_ids],
        proj_near[local_ids // M],
        preferred_element_type=jnp.float32,
    )
    environ = (cutoff[local_ids][..., None] * picked).astype(jnp.bfloat16)
    slots = environ.shape[1]
    owner_total = lax.axis_size("gx") * lax.axis_size("gy")
    capacity = max(2, 2 * flag_total // owner_total)
    same = (owner[:, None] == jnp.arange(owner_total, dtype=jnp.int32)[None, :]).astype(jnp.int32)
    before = jnp.cumsum(same, axis=0) - same
    slot_index = jnp.sum(before * same, axis=1)
    target = jnp.where(live_rows, owner * capacity + slot_index, owner_total * capacity)
    source_row = (
        jnp.full((owner_total * capacity,), flag_total, jnp.int32)
        .at[target]
        .set(jnp.arange(flag_total, dtype=jnp.int32), mode="drop")
    )
    padded_environ = jnp.concatenate(
        [environ, jnp.zeros((1, slots, env_width), environ.dtype)], axis=0
    )
    outgoing = padded_environ[source_row]
    local_first = w_first[0]
    local_head = w_head[0]
    results = specialist(
        lax.all_to_all(
            outgoing.reshape(owner_total, capacity, slots, env_width),
            ("gx", "gy"),
            split_axis=0,
            concat_axis=0,
            tiled=True,
        ),
        local_first,
        local_head,
    )
    returned = lax.all_to_all(results, ("gx", "gy"), split_axis=0, concat_axis=0, tiled=True)
    returned = returned.reshape(owner_total * capacity, 3)
    correction = returned[jnp.minimum(target, owner_total * capacity - 1)] * live_rows[
        :, None
    ].astype(jnp.float32)
    forces = base_force.at[:, local_ids].add(correction.T)
    return forces.reshape(3, cells_x, cells_y, depth)


def solution(mesh):
    placed = (
        P("gx", "gy", "gz", None),
        P("gx", "gy", "gz", None),
        P("gx", "gy", "gz", None),
        P(),
        P(),
        P(),
        P(),
        P(),
        P(("gx", "gy"), None, None),
        P(("gx", "gy"), None, None),
        P("gx", "gy", "gz", None),
        P("gx", "gy", "gz", None, None),
        P("gx", "gy", "gz"),
    )
    return jax.shard_map(
        per_device, mesh=mesh, in_specs=placed, out_specs=P(None, "gx", "gy", "gz"), check_vma=False
    )
```

```python
import math

import jax
import jax.numpy as jnp
from jax import lax
from jax.sharding import PartitionSpec as P
from jax.experimental import pallas as pl

M = 4
NRB = 8
L = 2


CUTOFF_RADIUS = 5.0
WIDTH_GAMMA = 2.0


def with_halo(cells, sides, width, closed):
    for axis, dim in sides:
        count = lax.axis_size(axis)
        ends = count if closed else count - 1
        head = lax.slice_in_dim(cells, 0, width, axis=dim)
        tail = lax.slice_in_dim(cells, cells.shape[dim] - width, cells.shape[dim], axis=dim)
        cells = jnp.concatenate(
            [
                lax.ppermute(tail, axis, [(i, (i + 1) % count) for i in range(ends)]),
                cells,
                lax.ppermute(head, axis, [((i + 1) % count, i) for i in range(ends)]),
            ],
            axis=dim,
        )
    return cells


def radial(distance):
    cutoff = 0.5 * (jnp.cos(jnp.pi * distance / CUTOFF_RADIUS) + 1.0)
    centres = 0.8 + jnp.arange(NRB).astype(distance.dtype) * (4.0 / (NRB - 1))
    radial_basis = jnp.exp(-WIDTH_GAMMA * (distance[..., None] - centres) ** 2) * cutoff[..., None]
    return (radial_basis.astype(jnp.bfloat16), cutoff)


def neighbour_rows(codes, coord_x, coord_y, coord_z, span_y, span_z):
    offset = codes // M
    within = codes % M
    step_x = offset // 9 - 1
    step_y = offset // 3 % 3 - 1
    step_z = offset % 3 - 1
    return (
        ((coord_x + 1 + step_x) * span_y + (coord_y + 1 + step_y)) * span_z
        + (coord_z // M + 1 + step_z) * M
        + within
    )


def update(state, summed, w_message, w_update, gain):
    message = jnp.dot(summed, w_message, preferred_element_type=jnp.float32)
    active = jax.nn.silu(message).astype(jnp.bfloat16)
    residual = state.astype(jnp.float32) + jnp.dot(
        active, w_update, preferred_element_type=jnp.float32
    )
    inv_rms = lax.rsqrt(jnp.mean(residual * residual, axis=-1, keepdims=True) + 1e-06)
    return (residual * inv_rms * gain).astype(jnp.bfloat16)


def ghosts(values):
    wider = with_halo(values, (("gy", 1), ("gx", 0)), 1, True)
    return with_halo(wider, (("gz", 2),), M, False)


def candidates(padded, cells_x, cells_y, cells_z):
    feature_width = padded.shape[-1]
    pieces = []
    for step_x in range(3):
        for step_y in range(3):
            for step_z in range(3):
                piece = padded[
                    step_x : step_x + cells_x,
                    step_y : step_y + cells_y,
                    step_z * M : step_z * M + cells_z * M,
                ]
                pieces.append(piece.reshape(cells_x, cells_y, cells_z, M, feature_width))
    stacked = jnp.stack(pieces, axis=3)
    return stacked.reshape(cells_x * cells_y * cells_z, 27 * M, feature_width)


def cheap_layer(state, weights, w_message, w_update, gain):
    cells_x, cells_y, depth, feature_width = state.shape
    cells_z = depth // M
    cell_count = cells_x * cells_y * cells_z
    atom_count = cell_count * M
    nearby = candidates(ghosts(state), cells_x, cells_y, cells_z)
    summed = jnp.einsum(
        "bmkc,bcf->bmkf",
        weights.reshape(cell_count, M, NRB, 27 * M),
        nearby,
        preferred_element_type=jnp.float32,
    )
    summed = summed.reshape(atom_count, NRB * feature_width).astype(jnp.bfloat16)
    return update(
        state.reshape(atom_count, feature_width), summed, w_message, w_update, gain
    ).reshape(state.shape)


def specialist_kernel(env_ref, first_ref, head_ref, out_ref):
    piece = 128
    slots = env_ref.shape[0] // out_ref.shape[0]
    span = piece * slots
    column = lax.broadcasted_iota(jnp.int32, (piece, span), 1)
    row = lax.broadcasted_iota(jnp.int32, (piece, span), 0)
    pool = ((column >= row * slots) & (column < (row + 1) * slots)).astype(jnp.bfloat16)

    def body(index, carry):
        begin = pl.multiple_of(index * span, span)
        message = jnp.dot(
            env_ref[pl.ds(begin, span), :], first_ref[...], preferred_element_type=jnp.float32
        )
        hidden = jax.nn.silu(message).astype(jnp.bfloat16)
        pooled = jnp.dot(pool, hidden, preferred_element_type=jnp.float32)
        pooled = (pooled * (1.0 / slots)).astype(jnp.bfloat16)
        out_ref[pl.ds(pl.multiple_of(index * piece, piece), piece), :] = jnp.dot(
            pooled, head_ref[...], preferred_element_type=jnp.float32
        )
        return carry

    lax.fori_loop(0, out_ref.shape[0] // piece, body, 0)


def specialist(received, w_first, w_head):
    sources, item_count, slots, env_width = received.shape
    env_total = sources * item_count
    hidden_width = w_first.shape[-1]
    block = math.gcd(env_total, 128)
    head = jnp.zeros((hidden_width, 128), jnp.bfloat16).at[:, : w_head.shape[0]].set(w_head.T)
    results = pl.pallas_call(
        specialist_kernel,
        grid=(env_total // block,),
        in_specs=[
            pl.BlockSpec((block * slots, env_width), lambda i: (i, 0)),
            pl.BlockSpec((env_width, hidden_width), lambda i: (0, 0)),
            pl.BlockSpec((hidden_width, 128), lambda i: (0, 0)),
        ],
        out_specs=pl.BlockSpec((block, 128), lambda i: (i, 0)),
        out_shape=jax.ShapeDtypeStruct((env_total, 128), jnp.float32),
    )(received.reshape(env_total * slots, env_width), w_first, head)
    return results[:, : w_head.shape[0]].reshape(sources, item_count, w_head.shape[0])


def per_device(
    features,
    neighbour_code,
    distance,
    w_message,
    w_update,
    norm_gain,
    w_env,
    w_out,
    w_first,
    w_head,
    flag_ids,
    flag_owner,
    flag_count,
):
    cells_x, cells_y, depth, feature_width = features.shape
    cells_z = depth // M
    atom_count = cells_x * cells_y * depth
    codes = neighbour_code.reshape(atom_count, -1)
    radial_basis, cutoff = radial(distance.reshape(atom_count, -1))
    code_range = jnp.arange(27 * M, dtype=jnp.int32)
    onehot = (codes[:, :, None] == code_range[None, None, :]).astype(jnp.bfloat16)
    weights = jnp.einsum(
        "ask,asc->akc", radial_basis, onehot, preferred_element_type=jnp.float32
    ).astype(jnp.bfloat16)
    state = features
    for layer_index in range(L):
        state = cheap_layer(
            state,
            weights,
            w_message[layer_index],
            w_update[layer_index],
            norm_gain[layer_index],
        )
    flat_state = state.reshape(atom_count, feature_width)
    projected = jnp.dot(flat_state, w_env, preferred_element_type=jnp.float32).astype(jnp.bfloat16)
    env_width = projected.shape[-1]
    proj_near = candidates(
        ghosts(projected.reshape(cells_x, cells_y, depth, env_width)), cells_x, cells_y, cells_z
    )
    base_force = jnp.einsum("af,cf->ca", flat_state, w_out, preferred_element_type=jnp.float32)
    local_ids = flag_ids.reshape(-1)
    owner = flag_owner.reshape(-1)
    flag_total = local_ids.shape[0]
    live_rows = jnp.arange(flag_total, dtype=jnp.int32) < flag_count.reshape(())
    picked = jnp.einsum(
        "rsc,rce->rse",
        onehot[local_ids],
        proj_near[local_ids // M],
        preferred_element_type=jnp.float32,
    )
    environ = (cutoff[local_ids][..., None] * picked).astype(jnp.bfloat16)
    slots = environ.shape[1]
    owner_total = lax.axis_size("gx") * lax.axis_size("gy")
    capacity = max(2, 2 * flag_total // owner_total)
    same = (owner[:, None] == jnp.arange(owner_total, dtype=jnp.int32)[None, :]).astype(jnp.int32)
    before = jnp.cumsum(same, axis=0) - same
    slot_index = jnp.sum(before * same, axis=1)
    target = jnp.where(live_rows, owner * capacity + slot_index, owner_total * capacity)
    source_row = (
        jnp.full((owner_total * capacity,), flag_total, jnp.int32)
        .at[target]
        .set(jnp.arange(flag_total, dtype=jnp.int32), mode="drop")
    )
    padded_environ = jnp.concatenate(
        [environ, jnp.zeros((1, slots, env_width), environ.dtype)], axis=0
    )
    outgoing = padded_environ[source_row]
    local_first = w_first[0]
    local_head = w_head[0]
    results = specialist(
        lax.all_to_all(
            outgoing.reshape(owner_total, capacity, slots, env_width),
            ("gx", "gy"),
            split_axis=0,
            concat_axis=0,
            tiled=True,
        ),
        local_first,
        local_head,
    )
    returned = lax.all_to_all(results, ("gx", "gy"), split_axis=0, concat_axis=0, tiled=True)
    returned = returned.reshape(owner_total * capacity, 3)
    correction = returned[jnp.minimum(target, owner_total * capacity - 1)] * live_rows[
        :, None
    ].astype(jnp.float32)
    forces = base_force.at[:, local_ids].add(correction.T)
    return forces.reshape(3, cells_x, cells_y, depth)


def solution(mesh):
    placed = (
        P("gx", "gy", "gz", None),
        P("gx", "gy", "gz", None),
        P("gx", "gy", "gz", None),
        P(),
        P(),
        P(),
        P(),
        P(),
        P(("gx", "gy"), None, None),
        P(("gx", "gy"), None, None),
        P("gx", "gy", "gz", None),
        P("gx", "gy", "gz", None, None),
        P("gx", "gy", "gz"),
    )
    return jax.shard_map(
        per_device, mesh=mesh, in_specs=placed, out_specs=P(None, "gx", "gy", "gz"), check_vma=False
    )
```

```python
import math

import jax
import jax.numpy as jnp
from jax import lax
from jax.sharding import PartitionSpec as P
from jax.experimental import pallas as pl

M = 4
NRB = 8
L = 2


CUTOFF_RADIUS = 5.0
WIDTH_GAMMA = 2.0


def with_halo(cells, sides, width, closed):
    for axis, dim in sides:
        count = lax.axis_size(axis)
        ends = count if closed else count - 1
        head = lax.slice_in_dim(cells, 0, width, axis=dim)
        tail = lax.slice_in_dim(cells, cells.shape[dim] - width, cells.shape[dim], axis=dim)
        cells = jnp.concatenate(
            [
                lax.ppermute(tail, axis, [(i, (i + 1) % count) for i in range(ends)]),
                cells,
                lax.ppermute(head, axis, [((i + 1) % count, i) for i in range(ends)]),
            ],
            axis=dim,
        )
    return cells


def radial(distance):
    cutoff = 0.5 * (jnp.cos(jnp.pi * distance / CUTOFF_RADIUS) + 1.0)
    centres = 0.8 + jnp.arange(NRB).astype(distance.dtype) * (4.0 / (NRB - 1))
    radial_basis = jnp.exp(-WIDTH_GAMMA * (distance[..., None] - centres) ** 2) * cutoff[..., None]
    return (radial_basis.astype(jnp.bfloat16), cutoff)


def neighbour_rows(codes, coord_x, coord_y, coord_z, span_y, span_z):
    offset = codes // M
    within = codes % M
    step_x = offset // 9 - 1
    step_y = offset // 3 % 3 - 1
    step_z = offset % 3 - 1
    return (
        ((coord_x + 1 + step_x) * span_y + (coord_y + 1 + step_y)) * span_z
        + (coord_z // M + 1 + step_z) * M
        + within
    )


def update(state, summed, w_message, w_update, gain):
    message = jnp.dot(summed, w_message, preferred_element_type=jnp.float32)
    active = jax.nn.silu(message).astype(jnp.bfloat16)
    residual = state.astype(jnp.float32) + jnp.dot(
        active, w_update, preferred_element_type=jnp.float32
    )
    inv_rms = lax.rsqrt(jnp.mean(residual * residual, axis=-1, keepdims=True) + 1e-06)
    return (residual * inv_rms * gain).astype(jnp.bfloat16)


def ghosts(values):
    wider = with_halo(values, (("gy", 1), ("gx", 0)), 1, True)
    return with_halo(wider, (("gz", 2),), M, False)


def candidates(padded, cells_x, cells_y, cells_z):
    feature_width = padded.shape[-1]
    deep = jnp.stack(
        [padded[:, :, step * M : step * M + cells_z * M] for step in range(3)], axis=2
    ).reshape(cells_x + 2, cells_y + 2, 3, cells_z, M, feature_width)
    wide = jnp.stack([deep[:, step : step + cells_y] for step in range(3)], axis=1)
    full = jnp.stack([wide[step : step + cells_x] for step in range(3)], axis=0)
    full = jnp.transpose(full, (1, 3, 5, 0, 2, 4, 6, 7))
    return full.reshape(cells_x * cells_y * cells_z, 27 * M, feature_width)


def cheap_layer(state, weights, w_message, w_update, gain):
    cells_x, cells_y, depth, feature_width = state.shape
    cells_z = depth // M
    cell_count = cells_x * cells_y * cells_z
    atom_count = cell_count * M
    nearby = candidates(ghosts(state), cells_x, cells_y, cells_z)
    summed = jnp.einsum(
        "bmkc,bcf->bmkf",
        weights.reshape(cell_count, M, NRB, 27 * M),
        nearby,
        preferred_element_type=jnp.float32,
    )
    summed = summed.reshape(atom_count, NRB * feature_width).astype(jnp.bfloat16)
    return update(
        state.reshape(atom_count, feature_width), summed, w_message, w_update, gain
    ).reshape(state.shape)


def specialist_kernel(env_ref, first_ref, head_ref, out_ref):
    piece = 64
    slots = env_ref.shape[0] // out_ref.shape[0]
    span = piece * slots
    column = lax.broadcasted_iota(jnp.int32, (piece, span), 1)
    row = lax.broadcasted_iota(jnp.int32, (piece, span), 0)
    pool = ((column >= row * slots) & (column < (row + 1) * slots)).astype(jnp.bfloat16)

    def body(index, carry):
        begin = pl.multiple_of(index * span, span)
        message = jnp.dot(
            env_ref[pl.ds(begin, span), :], first_ref[...], preferred_element_type=jnp.float32
        )
        hidden = jax.nn.silu(message).astype(jnp.bfloat16)
        pooled = jnp.dot(pool, hidden, preferred_element_type=jnp.float32)
        pooled = (pooled * (1.0 / slots)).astype(jnp.bfloat16)
        out_ref[pl.ds(pl.multiple_of(index * piece, piece), piece), :] = jnp.dot(
            pooled, head_ref[...], preferred_element_type=jnp.float32
        )
        return carry

    lax.fori_loop(0, out_ref.shape[0] // piece, body, 0)


def specialist(received, w_first, w_head):
    sources, item_count, slots, env_width = received.shape
    env_total = sources * item_count
    hidden_width = w_first.shape[-1]
    block = math.gcd(env_total, 64)
    head = jnp.zeros((hidden_width, 128), jnp.bfloat16).at[:, : w_head.shape[0]].set(w_head.T)
    results = pl.pallas_call(
        specialist_kernel,
        grid=(env_total // block,),
        in_specs=[
            pl.BlockSpec((block * slots, env_width), lambda i: (i, 0)),
            pl.BlockSpec((env_width, hidden_width), lambda i: (0, 0)),
            pl.BlockSpec((hidden_width, 128), lambda i: (0, 0)),
        ],
        out_specs=pl.BlockSpec((block, 128), lambda i: (i, 0)),
        out_shape=jax.ShapeDtypeStruct((env_total, 128), jnp.float32),
    )(received.reshape(env_total * slots, env_width), w_first, head)
    return results[:, : w_head.shape[0]].reshape(sources, item_count, w_head.shape[0])


def per_device(
    features,
    neighbour_code,
    distance,
    w_message,
    w_update,
    norm_gain,
    w_env,
    w_out,
    w_first,
    w_head,
    flag_ids,
    flag_owner,
    flag_count,
):
    cells_x, cells_y, depth, feature_width = features.shape
    cells_z = depth // M
    atom_count = cells_x * cells_y * depth
    codes = neighbour_code.reshape(atom_count, -1)
    radial_basis, cutoff = radial(distance.reshape(atom_count, -1))
    code_range = jnp.arange(27 * M, dtype=jnp.int32)
    onehot = (codes[:, :, None] == code_range[None, None, :]).astype(jnp.bfloat16)
    weights = jnp.einsum(
        "ask,asc->akc", radial_basis, onehot, preferred_element_type=jnp.float32
    ).astype(jnp.bfloat16)
    state = features
    for layer_index in range(L):
        state = cheap_layer(
            state,
            weights,
            w_message[layer_index],
            w_update[layer_index],
            norm_gain[layer_index],
        )
    flat_state = state.reshape(atom_count, feature_width)
    projected = jnp.dot(flat_state, w_env, preferred_element_type=jnp.float32).astype(jnp.bfloat16)
    env_width = projected.shape[-1]
    proj_near = candidates(
        ghosts(projected.reshape(cells_x, cells_y, depth, env_width)), cells_x, cells_y, cells_z
    )
    base_force = jnp.einsum("af,cf->ca", flat_state, w_out, preferred_element_type=jnp.float32)
    local_ids = flag_ids.reshape(-1)
    owner = flag_owner.reshape(-1)
    flag_total = local_ids.shape[0]
    live_rows = jnp.arange(flag_total, dtype=jnp.int32) < flag_count.reshape(())
    picked = jnp.einsum(
        "rsc,rce->rse",
        onehot[local_ids],
        proj_near[local_ids // M],
        preferred_element_type=jnp.float32,
    )
    environ = (cutoff[local_ids][..., None] * picked).astype(jnp.bfloat16)
    slots = environ.shape[1]
    owner_total = lax.axis_size("gx") * lax.axis_size("gy")
    capacity = max(2, 2 * flag_total // owner_total)
    same = (owner[:, None] == jnp.arange(owner_total, dtype=jnp.int32)[None, :]).astype(jnp.int32)
    before = jnp.cumsum(same, axis=0) - same
    slot_index = jnp.sum(before * same, axis=1)
    target = jnp.where(live_rows, owner * capacity + slot_index, owner_total * capacity)
    placing = (
        jnp.arange(owner_total * capacity, dtype=jnp.int32)[:, None] == target[None, :]
    ).astype(jnp.bfloat16)
    outgoing = jnp.dot(
        placing, environ.reshape(flag_total, slots * env_width), preferred_element_type=jnp.float32
    ).astype(jnp.bfloat16)
    local_first = w_first[0]
    local_head = w_head[0]
    results = specialist(
        lax.all_to_all(
            outgoing.reshape(owner_total, capacity, slots, env_width),
            ("gx", "gy"),
            split_axis=0,
            concat_axis=0,
            tiled=True,
        ),
        local_first,
        local_head,
    )
    returned = lax.all_to_all(results, ("gx", "gy"), split_axis=0, concat_axis=0, tiled=True)
    returned = returned.reshape(owner_total * capacity, 3)
    correction = returned[jnp.minimum(target, owner_total * capacity - 1)] * live_rows[
        :, None
    ].astype(jnp.float32)
    forces = base_force.at[:, local_ids].add(correction.T)
    return forces.reshape(3, cells_x, cells_y, depth)


def solution(mesh):
    placed = (
        P("gx", "gy", "gz", None),
        P("gx", "gy", "gz", None),
        P("gx", "gy", "gz", None),
        P(),
        P(),
        P(),
        P(),
        P(),
        P(("gx", "gy"), None, None),
        P(("gx", "gy"), None, None),
        P("gx", "gy", "gz", None),
        P("gx", "gy", "gz", None, None),
        P("gx", "gy", "gz"),
    )
    return jax.shard_map(
        per_device, mesh=mesh, in_specs=placed, out_specs=P(None, "gx", "gy", "gz"), check_vma=False
    )
```

```python
import math

import jax
import jax.numpy as jnp
from jax import lax
from jax.sharding import PartitionSpec as P
from jax.experimental import pallas as pl

M = 4
NRB = 8
L = 2


CUTOFF_RADIUS = 5.0
WIDTH_GAMMA = 2.0


def with_halo(cells, sides, width, closed):
    for axis, dim in sides:
        count = lax.axis_size(axis)
        ends = count if closed else count - 1
        head = lax.slice_in_dim(cells, 0, width, axis=dim)
        tail = lax.slice_in_dim(cells, cells.shape[dim] - width, cells.shape[dim], axis=dim)
        cells = jnp.concatenate(
            [
                lax.ppermute(tail, axis, [(i, (i + 1) % count) for i in range(ends)]),
                cells,
                lax.ppermute(head, axis, [((i + 1) % count, i) for i in range(ends)]),
            ],
            axis=dim,
        )
    return cells


def radial(distance):
    cutoff = 0.5 * (jnp.cos(jnp.pi * distance / CUTOFF_RADIUS) + 1.0)
    centres = 0.8 + jnp.arange(NRB).astype(distance.dtype) * (4.0 / (NRB - 1))
    radial_basis = jnp.exp(-WIDTH_GAMMA * (distance[..., None] - centres) ** 2) * cutoff[..., None]
    return (radial_basis.astype(jnp.bfloat16), cutoff)


def neighbour_rows(codes, coord_x, coord_y, coord_z, span_y, span_z):
    offset = codes // M
    within = codes % M
    step_x = offset // 9 - 1
    step_y = offset // 3 % 3 - 1
    step_z = offset % 3 - 1
    return (
        ((coord_x + 1 + step_x) * span_y + (coord_y + 1 + step_y)) * span_z
        + (coord_z // M + 1 + step_z) * M
        + within
    )


def update(state, summed, w_message, w_update, gain):
    message = jnp.dot(summed, w_message, preferred_element_type=jnp.float32)
    active = jax.nn.silu(message).astype(jnp.bfloat16)
    residual = state.astype(jnp.float32) + jnp.dot(
        active, w_update, preferred_element_type=jnp.float32
    )
    inv_rms = lax.rsqrt(jnp.mean(residual * residual, axis=-1, keepdims=True) + 1e-06)
    return (residual * inv_rms * gain).astype(jnp.bfloat16)


def ghosts(values):
    deeper = with_halo(values, (("gz", 2),), M, False)
    return with_halo(deeper, (("gy", 1), ("gx", 0)), 1, True)


def candidates(padded, cells_x, cells_y, cells_z):
    feature_width = padded.shape[-1]
    pieces = []
    for step_x in range(3):
        for step_y in range(3):
            for step_z in range(3):
                piece = padded[
                    step_x : step_x + cells_x,
                    step_y : step_y + cells_y,
                    step_z * M : step_z * M + cells_z * M,
                ]
                pieces.append(piece.reshape(cells_x, cells_y, cells_z, M, feature_width))
    stacked = jnp.stack(pieces, axis=3)
    return stacked.reshape(cells_x * cells_y * cells_z, 27 * M, feature_width)


def cheap_layer(state, weights, w_message, w_update, gain):
    cells_x, cells_y, depth, feature_width = state.shape
    cells_z = depth // M
    cell_count = cells_x * cells_y * cells_z
    atom_count = cell_count * M
    nearby = candidates(ghosts(state), cells_x, cells_y, cells_z)
    summed = jnp.einsum(
        "bmkc,bcf->bmkf",
        weights.reshape(cell_count, M, NRB, 27 * M),
        nearby,
        preferred_element_type=jnp.float32,
    )
    summed = summed.reshape(atom_count, NRB * feature_width).astype(jnp.bfloat16)
    return update(
        state.reshape(atom_count, feature_width), summed, w_message, w_update, gain
    ).reshape(state.shape)


def specialist_kernel(env_ref, first_ref, head_ref, out_ref):
    piece = 64
    slots = env_ref.shape[0] // out_ref.shape[0]
    span = piece * slots
    column = lax.broadcasted_iota(jnp.int32, (piece, span), 1)
    row = lax.broadcasted_iota(jnp.int32, (piece, span), 0)
    pool = ((column >= row * slots) & (column < (row + 1) * slots)).astype(jnp.bfloat16)

    def body(index, carry):
        begin = pl.multiple_of(index * span, span)
        message = jnp.dot(
            env_ref[pl.ds(begin, span), :], first_ref[...], preferred_element_type=jnp.float32
        )
        hidden = jax.nn.silu(message).astype(jnp.bfloat16)
        pooled = jnp.dot(pool, hidden, preferred_element_type=jnp.float32)
        pooled = (pooled * (1.0 / slots)).astype(jnp.bfloat16)
        out_ref[pl.ds(pl.multiple_of(index * piece, piece), piece), :] = jnp.dot(
            pooled, head_ref[...], preferred_element_type=jnp.float32
        )
        return carry

    lax.fori_loop(0, out_ref.shape[0] // piece, body, 0)


def specialist(received, w_first, w_head):
    sources, item_count, slots, env_width = received.shape
    env_total = sources * item_count
    hidden_width = w_first.shape[-1]
    block = math.gcd(env_total, 64)
    head = jnp.zeros((hidden_width, 128), jnp.bfloat16).at[:, : w_head.shape[0]].set(w_head.T)
    results = pl.pallas_call(
        specialist_kernel,
        grid=(env_total // block,),
        in_specs=[
            pl.BlockSpec((block * slots, env_width), lambda i: (i, 0)),
            pl.BlockSpec((env_width, hidden_width), lambda i: (0, 0)),
            pl.BlockSpec((hidden_width, 128), lambda i: (0, 0)),
        ],
        out_specs=pl.BlockSpec((block, 128), lambda i: (i, 0)),
        out_shape=jax.ShapeDtypeStruct((env_total, 128), jnp.float32),
    )(received.reshape(env_total * slots, env_width), w_first, head)
    return results[:, : w_head.shape[0]].reshape(sources, item_count, w_head.shape[0])


def per_device(
    features,
    neighbour_code,
    distance,
    w_message,
    w_update,
    norm_gain,
    w_env,
    w_out,
    w_first,
    w_head,
    flag_ids,
    flag_owner,
    flag_count,
):
    cells_x, cells_y, depth, feature_width = features.shape
    cells_z = depth // M
    atom_count = cells_x * cells_y * depth
    codes = neighbour_code.reshape(atom_count, -1)
    radial_basis, cutoff = radial(distance.reshape(atom_count, -1))
    code_range = jnp.arange(27 * M, dtype=jnp.int32)
    onehot = (codes[:, :, None] == code_range[None, None, :]).astype(jnp.bfloat16)
    weights = jnp.einsum(
        "ask,asc->akc", radial_basis, onehot, preferred_element_type=jnp.float32
    ).astype(jnp.bfloat16)
    state = features
    for layer_index in range(L):
        state = cheap_layer(
            state,
            weights,
            w_message[layer_index],
            w_update[layer_index],
            norm_gain[layer_index],
        )
    flat_state = state.reshape(atom_count, feature_width)
    projected = jnp.dot(flat_state, w_env, preferred_element_type=jnp.float32).astype(jnp.bfloat16)
    env_width = projected.shape[-1]
    proj_near = candidates(
        ghosts(projected.reshape(cells_x, cells_y, depth, env_width)), cells_x, cells_y, cells_z
    )
    base_force = jnp.einsum("af,cf->ca", flat_state, w_out, preferred_element_type=jnp.float32)
    local_ids = flag_ids.reshape(-1)
    owner = flag_owner.reshape(-1)
    flag_total = local_ids.shape[0]
    live_rows = jnp.arange(flag_total, dtype=jnp.int32) < flag_count.reshape(())
    picked = jnp.einsum(
        "rsc,rce->rse",
        onehot[local_ids],
        proj_near[local_ids // M],
        preferred_element_type=jnp.float32,
    )
    environ = (cutoff[local_ids][..., None] * picked).astype(jnp.bfloat16)
    slots = environ.shape[1]
    owner_total = lax.axis_size("gx") * lax.axis_size("gy")
    capacity = max(2, 2 * flag_total // owner_total)
    same = (owner[:, None] == jnp.arange(owner_total, dtype=jnp.int32)[None, :]).astype(jnp.int32)
    before = jnp.cumsum(same, axis=0) - same
    slot_index = jnp.sum(before * same, axis=1)
    target = jnp.where(live_rows, owner * capacity + slot_index, owner_total * capacity)
    placing = (
        jnp.arange(owner_total * capacity, dtype=jnp.int32)[:, None] == target[None, :]
    ).astype(jnp.bfloat16)
    outgoing = jnp.dot(
        placing, environ.reshape(flag_total, slots * env_width), preferred_element_type=jnp.float32
    ).astype(jnp.bfloat16)
    local_first = w_first[0]
    local_head = w_head[0]
    results = specialist(
        lax.all_to_all(
            outgoing.reshape(owner_total, capacity, slots, env_width),
            ("gx", "gy"),
            split_axis=0,
            concat_axis=0,
            tiled=True,
        ),
        local_first,
        local_head,
    )
    returned = lax.all_to_all(results, ("gx", "gy"), split_axis=0, concat_axis=0, tiled=True)
    returned = returned.reshape(owner_total * capacity, 3)
    correction = returned[jnp.minimum(target, owner_total * capacity - 1)] * live_rows[
        :, None
    ].astype(jnp.float32)
    forces = base_force.at[:, local_ids].add(correction.T)
    return forces.reshape(3, cells_x, cells_y, depth)


def solution(mesh):
    placed = (
        P("gx", "gy", "gz", None),
        P("gx", "gy", "gz", None),
        P("gx", "gy", "gz", None),
        P(),
        P(),
        P(),
        P(),
        P(),
        P(("gx", "gy"), None, None),
        P(("gx", "gy"), None, None),
        P("gx", "gy", "gz", None),
        P("gx", "gy", "gz", None, None),
        P("gx", "gy", "gz"),
    )
    return jax.shard_map(
        per_device, mesh=mesh, in_specs=placed, out_specs=P(None, "gx", "gy", "gz"), check_vma=False
    )
```

```python
import math

import jax
import jax.numpy as jnp
from jax import lax
from jax.sharding import PartitionSpec as P
from jax.experimental import pallas as pl

M = 4
NRB = 8
L = 2


CUTOFF_RADIUS = 5.0
WIDTH_GAMMA = 2.0


def with_halo(cells, sides, width, closed):
    for axis, dim in sides:
        count = lax.axis_size(axis)
        ends = count if closed else count - 1
        head = lax.slice_in_dim(cells, 0, width, axis=dim)
        tail = lax.slice_in_dim(cells, cells.shape[dim] - width, cells.shape[dim], axis=dim)
        cells = jnp.concatenate(
            [
                lax.ppermute(tail, axis, [(i, (i + 1) % count) for i in range(ends)]),
                cells,
                lax.ppermute(head, axis, [((i + 1) % count, i) for i in range(ends)]),
            ],
            axis=dim,
        )
    return cells


def radial(distance):
    cutoff = 0.5 * (jnp.cos(jnp.pi * distance / CUTOFF_RADIUS) + 1.0)
    centres = 0.8 + jnp.arange(NRB).astype(distance.dtype) * (4.0 / (NRB - 1))
    radial_basis = jnp.exp(-WIDTH_GAMMA * (distance[..., None] - centres) ** 2) * cutoff[..., None]
    return (radial_basis.astype(jnp.bfloat16), cutoff)


def neighbour_rows(codes, coord_x, coord_y, coord_z, span_y, span_z):
    offset = codes // M
    within = codes % M
    step_x = offset // 9 - 1
    step_y = offset // 3 % 3 - 1
    step_z = offset % 3 - 1
    return (
        ((coord_x + 1 + step_x) * span_y + (coord_y + 1 + step_y)) * span_z
        + (coord_z // M + 1 + step_z) * M
        + within
    )


def update(state, summed, w_message, w_update, gain):
    message = jnp.dot(summed, w_message, preferred_element_type=jnp.float32)
    active = jax.nn.silu(message).astype(jnp.bfloat16)
    residual = state.astype(jnp.float32) + jnp.dot(
        active, w_update, preferred_element_type=jnp.float32
    )
    inv_rms = lax.rsqrt(jnp.mean(residual * residual, axis=-1, keepdims=True) + 1e-06)
    return (residual * inv_rms * gain).astype(jnp.bfloat16)


def ghosts(values):
    deeper = with_halo(values, (("gz", 2),), M, False)
    return with_halo(deeper, (("gy", 1), ("gx", 0)), 1, True)


def candidates(padded, cells_x, cells_y, cells_z):
    feature_width = padded.shape[-1]
    pieces = []
    for step_x in range(3):
        for step_y in range(3):
            for step_z in range(3):
                piece = padded[
                    step_x : step_x + cells_x,
                    step_y : step_y + cells_y,
                    step_z * M : step_z * M + cells_z * M,
                ]
                pieces.append(piece.reshape(cells_x, cells_y, cells_z, M, feature_width))
    stacked = jnp.stack(pieces, axis=3)
    return stacked.reshape(cells_x * cells_y * cells_z, 27 * M, feature_width)


def cheap_layer(state, weights, w_message, w_update, gain):
    cells_x, cells_y, depth, feature_width = state.shape
    cells_z = depth // M
    cell_count = cells_x * cells_y * cells_z
    atom_count = cell_count * M
    nearby = candidates(ghosts(state), cells_x, cells_y, cells_z)
    summed = jnp.einsum(
        "bmkc,bcf->bmkf",
        weights.reshape(cell_count, M, NRB, 27 * M),
        nearby,
        preferred_element_type=jnp.float32,
    )
    summed = summed.reshape(atom_count, NRB * feature_width).astype(jnp.bfloat16)
    return update(
        state.reshape(atom_count, feature_width), summed, w_message, w_update, gain
    ).reshape(state.shape)


def specialist_kernel(env_ref, first_ref, head_ref, out_ref):
    piece = 128
    slots = env_ref.shape[0] // out_ref.shape[0]
    span = piece * slots
    column = lax.broadcasted_iota(jnp.int32, (piece, span), 1)
    row = lax.broadcasted_iota(jnp.int32, (piece, span), 0)
    pool = ((column >= row * slots) & (column < (row + 1) * slots)).astype(jnp.bfloat16)

    def body(index, carry):
        begin = pl.multiple_of(index * span, span)
        message = jnp.dot(
            env_ref[pl.ds(begin, span), :], first_ref[...], preferred_element_type=jnp.float32
        )
        hidden = jax.nn.silu(message).astype(jnp.bfloat16)
        pooled = jnp.dot(pool, hidden, preferred_element_type=jnp.float32)
        pooled = (pooled * (1.0 / slots)).astype(jnp.bfloat16)
        out_ref[pl.ds(pl.multiple_of(index * piece, piece), piece), :] = jnp.dot(
            pooled, head_ref[...], preferred_element_type=jnp.float32
        )
        return carry

    lax.fori_loop(0, out_ref.shape[0] // piece, body, 0)


def specialist(received, w_first, w_head):
    sources, item_count, slots, env_width = received.shape
    env_total = sources * item_count
    hidden_width = w_first.shape[-1]
    block = math.gcd(env_total, 128)
    head = jnp.zeros((hidden_width, 128), jnp.bfloat16).at[:, : w_head.shape[0]].set(w_head.T)
    results = pl.pallas_call(
        specialist_kernel,
        grid=(env_total // block,),
        in_specs=[
            pl.BlockSpec((block * slots, env_width), lambda i: (i, 0)),
            pl.BlockSpec((env_width, hidden_width), lambda i: (0, 0)),
            pl.BlockSpec((hidden_width, 128), lambda i: (0, 0)),
        ],
        out_specs=pl.BlockSpec((block, 128), lambda i: (i, 0)),
        out_shape=jax.ShapeDtypeStruct((env_total, 128), jnp.float32),
    )(received.reshape(env_total * slots, env_width), w_first, head)
    return results[:, : w_head.shape[0]].reshape(sources, item_count, w_head.shape[0])


def per_device(
    features,
    neighbour_code,
    distance,
    w_message,
    w_update,
    norm_gain,
    w_env,
    w_out,
    w_first,
    w_head,
    flag_ids,
    flag_owner,
    flag_count,
):
    cells_x, cells_y, depth, feature_width = features.shape
    cells_z = depth // M
    atom_count = cells_x * cells_y * depth
    codes = neighbour_code.reshape(atom_count, -1)
    radial_basis, cutoff = radial(distance.reshape(atom_count, -1))
    code_range = jnp.arange(27 * M, dtype=jnp.int32)
    onehot = (codes[:, :, None] == code_range[None, None, :]).astype(jnp.bfloat16)
    weights = jnp.einsum(
        "ask,asc->akc", radial_basis, onehot, preferred_element_type=jnp.float32
    ).astype(jnp.bfloat16)
    state = features
    for layer_index in range(L):
        state = cheap_layer(
            state,
            weights,
            w_message[layer_index],
            w_update[layer_index],
            norm_gain[layer_index],
        )
    flat_state = state.reshape(atom_count, feature_width)
    projected = jnp.dot(flat_state, w_env, preferred_element_type=jnp.float32).astype(jnp.bfloat16)
    env_width = projected.shape[-1]
    proj_near = candidates(
        ghosts(projected.reshape(cells_x, cells_y, depth, env_width)), cells_x, cells_y, cells_z
    )
    base_force = jnp.einsum("af,cf->ca", flat_state, w_out, preferred_element_type=jnp.float32)
    local_ids = flag_ids.reshape(-1)
    owner = flag_owner.reshape(-1)
    flag_total = local_ids.shape[0]
    live_rows = jnp.arange(flag_total, dtype=jnp.int32) < flag_count.reshape(())
    picked = jnp.einsum(
        "rsc,rce->rse",
        onehot[local_ids],
        proj_near[local_ids // M],
        preferred_element_type=jnp.float32,
    )
    environ = (cutoff[local_ids][..., None] * picked).astype(jnp.bfloat16)
    slots = environ.shape[1]
    owner_total = lax.axis_size("gx") * lax.axis_size("gy")
    capacity = max(2, 2 * flag_total // owner_total)
    same = (owner[:, None] == jnp.arange(owner_total, dtype=jnp.int32)[None, :]).astype(jnp.int32)
    before = jnp.cumsum(same, axis=0) - same
    slot_index = jnp.sum(before * same, axis=1)
    target = jnp.where(live_rows, owner * capacity + slot_index, owner_total * capacity)
    placing = (
        jnp.arange(owner_total * capacity, dtype=jnp.int32)[:, None] == target[None, :]
    ).astype(jnp.bfloat16)
    outgoing = jnp.dot(
        placing, environ.reshape(flag_total, slots * env_width), preferred_element_type=jnp.float32
    ).astype(jnp.bfloat16)
    local_first = w_first[0]
    local_head = w_head[0]
    results = specialist(
        lax.all_to_all(
            outgoing.reshape(owner_total, capacity, slots, env_width),
            ("gx", "gy"),
            split_axis=0,
            concat_axis=0,
            tiled=True,
        ),
        local_first,
        local_head,
    )
    returned = lax.all_to_all(results, ("gx", "gy"), split_axis=0, concat_axis=0, tiled=True)
    returned = returned.reshape(owner_total * capacity, 3)
    correction = returned[jnp.minimum(target, owner_total * capacity - 1)] * live_rows[
        :, None
    ].astype(jnp.float32)
    forces = base_force.at[:, local_ids].add(correction.T)
    return forces.reshape(3, cells_x, cells_y, depth)


def solution(mesh):
    placed = (
        P("gx", "gy", "gz", None),
        P("gx", "gy", "gz", None),
        P("gx", "gy", "gz", None),
        P(),
        P(),
        P(),
        P(),
        P(),
        P(("gx", "gy"), None, None),
        P(("gx", "gy"), None, None),
        P("gx", "gy", "gz", None),
        P("gx", "gy", "gz", None, None),
        P("gx", "gy", "gz"),
    )
    return jax.shard_map(
        per_device, mesh=mesh, in_specs=placed, out_specs=P(None, "gx", "gy", "gz"), check_vma=False
    )
```
